128 devices in a mesh: seq: 16 (over y, x_lo, core), tp: 8 (over z, x_hi).
Axes of the slice: x: 4 (x_hi: 2, x_lo: 2; x = x_hi * 2 + x_lo), y: 4, z: 4, core: 2. Of those that a mesh axis runs over, the one named last changes fastest.
Arguments:
- tokens: bfloat16 [8192, 4096], P('seq'), may hold values from -6 to 6
- norm_gain: bfloat16 [4096], replicated, may hold values from 0.099609375 to 1.8984375
- w_query: bfloat16 [4096, 4096], P(None, 'tp'), may hold values from -4 to 4
- w_key: bfloat16 [4096, 512], replicated, may hold values from -1 to 1
- w_value: bfloat16 [4096, 512], replicated, may hold values from -0.09375 to 0.09375
- w_out: bfloat16 [4096, 4096], P('tp'), may hold values from -0.375 to 0.375
- prompt_lengths: int32 [16], replicated, may hold values from 1 to 6144, 8192 in all
- page_slots: int32 [64], replicated, may hold values from 0 to 63, each once
Outputs:
- attended: bfloat16 [8192, 4096], P(('seq', 'tp'))
- kv_cache: bfloat16 [64, 128, 1024], P('seq', None, 'tp')
The draws below stay inside these ranges and needn't reach their ends.
Inputs may be any that keep to these rules, and one draw needn't show every extreme that they name: `prompt_lengths`: the lengths sum to 8192; the longest prompt has exactly 6144 tokens. `page_slots`: every value appears exactly once.
All inputs are finite; a program needn't handle non-finite values.
Results may differ from the reference program's by a relative error of at most 0.015.
Values may be sent and summed in bfloat16 or wider, within the bound.
No kernel may reach another device: no remote copies, remote signals or barrier semaphores. Data moves between devices by JAX's collectives and lax.ppermute only.
A program may use at most 128 MiB of HBM per device.

```python
import math
import jax
import jax.numpy as jnp
import numpy as np
from jax import lax

D = 4096
H = 32
KVH = 4
HD = 128
PAGE = 128
PROMPTS = 16
TOKENS = 8192
MAXLEN = 6144
PAGES = 64
N_TP = 8


def key_matrix(key):
    return jax.random.normal(jax.random.fold_in(key, 11), (D, KVH * HD), jnp.float32) / math.sqrt(D)


def draw_w_key(key, part):
    return key_matrix(key).astype(jnp.bfloat16)


def draw_w_query(key, part):
    drawn = jax.random.normal(jax.random.fold_in(key, 12), (D, H * HD), jnp.float32) / math.sqrt(D)
    return jnp.clip(drawn, -4.0, 4.0).astype(jnp.bfloat16)


def draw_tokens(key, part):
    drawn = jax.random.normal(jax.random.fold_in(key, 10), (TOKENS, D), jnp.float32)
    return jnp.clip(drawn, -6.0, 6.0).astype(jnp.bfloat16)


def shard_levels(own_key, dims, split, least, high):
    loudness = 1.0
    for axis_at, shards_of in split:
        heights = jax.random.uniform(jax.random.fold_in(jax.random.fold_in(own_key, 6), axis_at), (shards_of,), jnp.float32, least / len(split), high / len(split))
        loudness = loudness * jnp.repeat(jnp.exp(heights), dims[axis_at] // shards_of).reshape((-1,) + (1,) * (len(dims) - 1 - axis_at))
    return loudness


def split_up(number_of, total, limit, slope):
    loads = [(1 << 20) // math.isqrt(standing ** slope) + 1 for standing in range(2, number_of + 1)]
    spare, given = total - limit - (number_of - 1), [1] * (number_of - 1)
    while spare > 0:
        candidates = [i for i in range(number_of - 1) if given[i] < limit]
        whole, left = sum([loads[i] for i in candidates]), spare
        for i in candidates:
            more = min(limit - given[i], max(1, left * loads[i] // whole), spare)
            given[i] = given[i] + more
            spare = spare - more
    return np.array([limit] + given)


def uneven(own_key, amount, total, reach, skew):
    if amount == 2:
        one = jax.random.randint(own_key, (), max(1, total - reach), min(reach, total - 1) + 1)
        return jnp.stack([one, total - one])
    sizes = jnp.asarray(split_up(amount, total, reach, skew), jnp.int32)
    twos = (amount - 1) // 2
    donor, sink = sizes[1:1 + 2 * twos:2], sizes[2:2 + 2 * twos:2]
    room = jnp.minimum(donor - 1, reach - sink)
    shifted = jax.random.randint(jax.random.fold_in(own_key, 1), (twos,), 0, 1 << 20) % (room + 1)
    sizes = sizes.at[1:1 + 2 * twos:2].set(donor - shifted).at[2:2 + 2 * twos:2].set(sink + shifted)
    return sizes[jax.random.permutation(jax.random.fold_in(own_key, 2), amount)]


def bell_draw(rng, extent, spread, most, split=(), held_as=jnp.bfloat16):
    array = spread * jax.random.normal(rng, extent, jnp.float32)
    if split:
        array = array * shard_levels(rng, extent, split, -0.22, 0.18)
    return jnp.clip(array, -most, most).astype(held_as)


def setup_inputs(seed: int = 0) -> dict:
    arg_keys = jax.random.split(jax.random.key(seed), 9)
    tokens = draw_tokens(jax.random.fold_in(arg_keys[8], 71), 0)
    norm_gain = jnp.clip(1.0 + 0.18 * jax.random.normal(arg_keys[1], (D,), jnp.float32), 0.099609375, 1.8984375).astype(jnp.bfloat16)
    w_query = draw_w_query(jax.random.fold_in(arg_keys[8], 71), 0)
    w_key = draw_w_key(jax.random.fold_in(arg_keys[8], 71), 0)
    w_value = bell_draw(arg_keys[4], (D, KVH * HD), D ** -0.5, 0.09375)
    w_out = bell_draw(arg_keys[5], (H * HD, D), (D // 16) ** -0.5, 0.375, ((0, 8),))
    prompt_lengths = uneven(arg_keys[6], PROMPTS, TOKENS, MAXLEN, 2).astype(jnp.int32)
    page_slots = jax.random.permutation(arg_keys[7], PAGES).astype(jnp.int32)
    return dict(tokens=tokens, norm_gain=norm_gain, w_query=w_query, w_key=w_key, w_value=w_value, w_out=w_out, prompt_lengths=prompt_lengths, page_slots=page_slots)


epsilon = 1e-05
rope_base = 5000000.0

def segment_info(token_index, prompt_lengths):
    prompt_ends = jnp.cumsum(prompt_lengths).astype(jnp.int32)
    finished = prompt_ends[None, :] <= token_index[:, None]
    segment = lax.optimization_barrier(jnp.sum(finished.astype(jnp.int32), axis=1)).astype(jnp.int32)
    offset = lax.optimization_barrier(jnp.sum(jnp.where(finished, prompt_lengths[None, :], 0), axis=1)).astype(jnp.int32)
    return (segment, (token_index - offset).astype(jnp.int32))

def rotate(vectors, position):
    half_size = HD // 2
    frequency = rope_base ** (-(2.0 * jnp.arange(half_size, dtype=jnp.float32)) / HD)
    angle = position.astype(jnp.float32)[:, None] * frequency[None, :]
    cosine = jnp.cos(angle)[:, None, :]
    sine = jnp.sin(angle)[:, None, :]
    first_half = vectors[..., :half_size]
    second_half = vectors[..., half_size:]
    return jnp.concatenate([first_half * cosine - second_half * sine, second_half * cosine + first_half * sine], axis=-1)

def normalize(tokens, norm_gain):
    hidden = tokens.astype(jnp.float32)
    factor = lax.rsqrt(lax.optimization_barrier(jnp.mean(hidden * hidden, axis=-1, keepdims=True)) + epsilon)
    return (hidden * factor * norm_gain.astype(jnp.float32)).astype(jnp.bfloat16)

def reference(tokens, norm_gain, w_query, w_key, w_value, w_out, prompt_lengths, page_slots):
    token_index = jnp.arange(TOKENS, dtype=jnp.int32)
    segment, position = segment_info(token_index, prompt_lengths)
    normed = normalize(tokens, norm_gain)
    queries = rotate(jnp.dot(normed, w_query, preferred_element_type=jnp.float32).reshape(TOKENS, H, HD), position).astype(jnp.bfloat16)
    keys_all = rotate(jnp.dot(normed, w_key, preferred_element_type=jnp.float32).reshape(TOKENS, KVH, HD), position).astype(jnp.bfloat16)
    values_all = jnp.dot(normed, w_value, preferred_element_type=jnp.float32).astype(jnp.bfloat16).reshape(TOKENS, KVH, HD)
    block_rows = min(TOKENS, 1024)
    block_total = TOKENS // block_rows
    group_size = H // KVH
    score_scale = HD ** (-0.5)
    query_heads = queries.transpose(1, 0, 2).reshape(H, block_total, block_rows, HD)
    key_heads = keys_all.transpose(1, 0, 2)
    value_heads = values_all.transpose(1, 0, 2)

    def one_head(head_number):
        head_keys = key_heads[head_number // group_size]
        head_values = value_heads[head_number // group_size]

        def one_block(block_number):
            block_queries = query_heads[head_number, block_number]
            row_index = block_number * block_rows + jnp.arange(block_rows, dtype=jnp.int32)
            row_segment = lax.dynamic_slice_in_dim(segment, block_number * block_rows, block_rows)
            scores = jnp.dot(block_queries, head_keys.T, preferred_element_type=jnp.float32) * score_scale
            visible = (token_index[None, :] <= row_index[:, None]) & (segment[None, :] == row_segment[:, None])
            largest = lax.optimization_barrier(jnp.max(jnp.where(visible, scores, -1e+30), axis=1, keepdims=True))
            weights = jnp.where(visible, jnp.exp(scores - largest), 0.0)
            weight_sum = lax.optimization_barrier(jnp.sum(weights, axis=1, keepdims=True))
            weighted = jnp.dot(weights.astype(jnp.bfloat16), head_values, preferred_element_type=jnp.float32)
            return (weighted / weight_sum).astype(jnp.bfloat16)
        return lax.map(one_block, jnp.arange(block_total, dtype=jnp.int32))
    heads_out = lax.map(one_head, jnp.arange(H, dtype=jnp.int32))
    heads_out = heads_out.reshape(H, TOKENS, HD).transpose(1, 0, 2).reshape(TOKENS, H * HD)
    group_width = H * HD // N_TP
    summed = jnp.zeros((TOKENS, D), jnp.float32)
    for group_number in range(N_TP):
        partial_value = jnp.dot(heads_out[:, group_number * group_width:(group_number + 1) * group_width], w_out[group_number * group_width:(group_number + 1) * group_width], preferred_element_type=jnp.float32)
        partial_value = lax.optimization_barrier(partial_value.astype(jnp.bfloat16))
        summed = summed + partial_value.astype(jnp.float32)
    attended = summed.astype(jnp.bfloat16)
    page_rows = jnp.stack([keys_all, values_all], axis=2).reshape(PAGES, PAGE, KVH * 2 * HD)
    kv_cache = jnp.zeros_like(page_rows).at[page_slots].set(page_rows)
    return (attended, kv_cache)
```

```python
import functools

import jax
import jax.numpy as jnp
from jax import lax
from jax.experimental import pallas as pl
from jax.experimental.pallas import tpu as pltpu
from jax.sharding import PartitionSpec as P

HD = 128
PAGE = 128
BQ = 256
BK = 256


epsilon = 1e-05
rope_base = 5000000.0


def segment_start(token_index, prompt_lengths):
    prompt_ends = jnp.cumsum(prompt_lengths)
    finished = prompt_ends[None, :] <= token_index[:, None]
    return jnp.sum(jnp.where(finished, prompt_lengths[None, :], 0), axis=1)


def rotate(vectors, position):
    half_size = HD // 2
    frequency = rope_base ** (-(2.0 * jnp.arange(half_size, dtype=jnp.float32)) / HD)
    angle = position.astype(jnp.float32)[:, None] * frequency[None, :]
    cosine = jnp.cos(angle)[:, None, :]
    sine = jnp.sin(angle)[:, None, :]
    first_half = vectors[..., :half_size]
    second_half = vectors[..., half_size:]
    return jnp.concatenate(
        [first_half * cosine - second_half * sine, second_half * cosine + first_half * sine],
        axis=-1,
    )


def normalize(tokens, norm_gain):
    hidden = tokens.astype(jnp.float32)
    factor = lax.rsqrt(jnp.mean(hidden * hidden, axis=-1, keepdims=True) + epsilon)
    return (hidden * factor * norm_gain.astype(jnp.float32)).astype(jnp.bfloat16)


def flash_kernel(lo_ref, hi_ref, base_ref, q_ref, start_ref, kv_ref, o_ref):
    i = pl.program_id(0)
    q = q_ref[...]
    row_index = base_ref[i] + lax.broadcasted_iota(jnp.int32, (BQ, 1), 0)
    row_start = start_ref[...]
    scale = HD ** (-0.5)

    def body(kb, carry):
        running_max, running_sum, weighted = carry
        offset = pl.multiple_of(kb * BK, BK)
        keys = kv_ref[pl.ds(offset, BK), pl.ds(0, HD)]
        values = kv_ref[pl.ds(offset, BK), pl.ds(HD, HD)]
        scores = lax.dot_general(
            q, keys, (((1,), (1,)), ((), ())), preferred_element_type=jnp.float32
        ) * scale
        key_index = offset + lax.broadcasted_iota(jnp.int32, (1, BK), 1)
        visible = (key_index >= row_start) & (key_index <= row_index)
        fresh_max = jnp.maximum(
            running_max, jnp.max(jnp.where(visible, scores, -1e30), axis=1, keepdims=True)
        )
        weights = jnp.where(visible, jnp.exp(scores - fresh_max), 0.0)
        shrink = jnp.exp(running_max - fresh_max)
        running_sum = running_sum * shrink + jnp.sum(weights, axis=1, keepdims=True)
        weighted = weighted * shrink + jnp.dot(
            weights.astype(jnp.bfloat16), values, preferred_element_type=jnp.float32
        )
        return (fresh_max, running_sum, weighted)

    init = (
        jnp.full((BQ, 1), -1e30, jnp.float32),
        jnp.zeros((BQ, 1), jnp.float32),
        jnp.zeros((BQ, HD), jnp.float32),
    )
    running_max, running_sum, weighted = lax.fori_loop(lo_ref[i], hi_ref[i] + 1, body, init)
    o_ref[...] = (weighted / running_sum).astype(o_ref.dtype)


def flash_attention(queries, row_start, key_values, block_lo, block_hi, block_base):
    rows, width = queries.shape
    heads = width // HD
    q_blocks = rows // BQ
    kv_rows = key_values.shape[0]
    grid_spec = pltpu.PrefetchScalarGridSpec(
        num_scalar_prefetch=3,
        grid=(q_blocks, heads),
        in_specs=[
            pl.BlockSpec((BQ, HD), lambda i, h, lo, hi, base: (i, h)),
            pl.BlockSpec((BQ, 1), lambda i, h, lo, hi, base: (i, 0)),
            pl.BlockSpec((kv_rows, 2 * HD), lambda i, h, lo, hi, base: (0, 0)),
        ],
        out_specs=pl.BlockSpec((BQ, HD), lambda i, h, lo, hi, base: (i, h)),
    )
    return pl.pallas_call(
        flash_kernel,
        grid_spec=grid_spec,
        out_shape=jax.ShapeDtypeStruct((rows, width), jnp.bfloat16),
    )(block_lo, block_hi, block_base, queries, row_start, key_values)


def on_device(tokens, norm_gain, w_query, w_key, w_value, w_out, prompt_lengths, page_slots):
    row_count = tokens.shape[0]
    tp_count = lax.axis_size("tp")
    seq_rank = lax.axis_index("seq")
    tp_rank = lax.axis_index("tp")
    heads_here = w_query.shape[1] // HD
    kv_heads = w_key.shape[1] // HD
    sharing = tp_count // kv_heads
    kv_head = tp_rank // sharing
    token_index = seq_rank * row_count + jnp.arange(row_count, dtype=jnp.int32)
    start = segment_start(token_index, prompt_lengths)
    position = token_index - start
    normed = normalize(tokens, norm_gain)

    key_columns = lax.dynamic_slice_in_dim(w_key, kv_head * HD, HD, 1)
    value_columns = lax.dynamic_slice_in_dim(w_value, kv_head * HD, HD, 1)
    keys_here = rotate(
        jnp.dot(normed, key_columns, preferred_element_type=jnp.float32)[:, None, :], position
    )[:, 0].astype(jnp.bfloat16)
    values_here = jnp.dot(normed, value_columns, preferred_element_type=jnp.float32).astype(
        jnp.bfloat16
    )
    keys_values = jnp.concatenate([keys_here, values_here], axis=1)
    gathered = lax.all_gather(keys_values, "seq", axis=0, tiled=True)

    queries = rotate(
        jnp.dot(normed, w_query, preferred_element_type=jnp.float32).reshape(
            row_count, heads_here, HD
        ),
        position,
    ).astype(jnp.bfloat16).reshape(row_count, heads_here * HD)

    q_blocks = row_count // BQ
    first_rows = start.reshape(q_blocks, BQ)[:, 0]
    block_base = seq_rank * row_count + BQ * jnp.arange(q_blocks, dtype=jnp.int32)
    block_lo = first_rows // BK
    block_hi = (block_base + BQ - 1) // BK
    heads_out = flash_attention(
        queries, start[:, None], gathered, block_lo, block_hi, block_base
    )

    attended = lax.psum_scatter(
        jnp.dot(heads_out, w_out, preferred_element_type=jnp.float32).astype(jnp.bfloat16),
        "tp",
        scatter_dimension=0,
        tiled=True,
    )

    cache_width = 2 * HD // sharing
    cache_column = tp_rank % sharing * cache_width
    slots_here = row_count // PAGE
    page_total = page_slots.shape[0]
    wanted = seq_rank * slots_here + jnp.arange(slots_here, dtype=jnp.int32)
    page_of_slot = jnp.sum(
        jnp.where(
            page_slots[None, :] == wanted[:, None],
            jnp.arange(page_total, dtype=jnp.int32)[None, :],
            0,
        ),
        axis=1,
    )
    pages = [
        lax.dynamic_slice(gathered, (page_of_slot[j] * PAGE, cache_column), (PAGE, cache_width))
        for j in range(slots_here)
    ]
    cache_here = jnp.stack(pages, axis=0)
    return (attended, cache_here)


def solution(mesh):
    placed = (P("seq", None), P(), P(None, "tp"), P(), P(), P("tp", None), P(), P())
    return jax.shard_map(
        on_device,
        mesh=mesh,
        in_specs=placed,
        out_specs=(P(("seq", "tp"), None), P("seq", None, "tp")),
        check_vma=False,
    )
```

```python
import functools

import jax
import jax.numpy as jnp
from jax import lax
from jax.experimental import pallas as pl
from jax.experimental.pallas import tpu as pltpu
from jax.sharding import PartitionSpec as P

HD = 128
PAGE = 128
BQ = 256
BK = 256


epsilon = 1e-05
rope_base = 5000000.0


def segment_start(token_index, prompt_lengths):
    prompt_ends = jnp.cumsum(prompt_lengths)
    finished = prompt_ends[None, :] <= token_index[:, None]
    return jnp.sum(jnp.where(finished, prompt_lengths[None, :], 0), axis=1)


def rotate(vectors, position):
    half_size = HD // 2
    frequency = rope_base ** (-(2.0 * jnp.arange(half_size, dtype=jnp.float32)) / HD)
    angle = position.astype(jnp.float32)[:, None] * frequency[None, :]
    cosine = jnp.cos(angle)[:, None, :]
    sine = jnp.sin(angle)[:, None, :]
    first_half = vectors[..., :half_size]
    second_half = vectors[..., half_size:]
    return jnp.concatenate(
        [first_half * cosine - second_half * sine, second_half * cosine + first_half * sine],
        axis=-1,
    )


def normalize(tokens, norm_gain):
    hidden = tokens.astype(jnp.float32)
    factor = lax.rsqrt(jnp.mean(hidden * hidden, axis=-1, keepdims=True) + epsilon)
    return (hidden * factor * norm_gain.astype(jnp.float32)).astype(jnp.bfloat16)


def flash_kernel(lo_ref, hi_ref, base_ref, q_ref, start_ref, kv_ref, o_ref):
    i = pl.program_id(0)
    q = q_ref[...]
    row_index = base_ref[i] + lax.broadcasted_iota(jnp.int32, (BQ, 1), 0)
    row_start = start_ref[...]
    scale = HD ** (-0.5)

    def body(kb, carry):
        running_max, running_sum, weighted = carry
        offset = pl.multiple_of(kb * BK, BK)
        keys = kv_ref[pl.ds(offset, BK), pl.ds(0, HD)]
        values = kv_ref[pl.ds(offset, BK), pl.ds(HD, HD)]
        scores = lax.dot_general(
            q, keys, (((1,), (1,)), ((), ())), preferred_element_type=jnp.float32
        ) * scale
        key_index = offset + lax.broadcasted_iota(jnp.int32, (1, BK), 1)
        visible = (key_index >= row_start) & (key_index <= row_index)
        fresh_max = jnp.maximum(
            running_max, jnp.max(jnp.where(visible, scores, -1e30), axis=1, keepdims=True)
        )
        weights = jnp.where(visible, jnp.exp(scores - fresh_max), 0.0)
        shrink = jnp.exp(running_max - fresh_max)
        running_sum = running_sum * shrink + jnp.sum(weights, axis=1, keepdims=True)
        weighted = weighted * shrink + jnp.dot(
            weights.astype(jnp.bfloat16), values, preferred_element_type=jnp.float32
        )
        return (fresh_max, running_sum, weighted)

    init = (
        jnp.full((BQ, 1), -1e30, jnp.float32),
        jnp.zeros((BQ, 1), jnp.float32),
        jnp.zeros((BQ, HD), jnp.float32),
    )
    running_max, running_sum, weighted = lax.fori_loop(lo_ref[i], hi_ref[i] + 1, body, init)
    o_ref[...] = (weighted / running_sum).astype(o_ref.dtype)


def flash_attention(queries, row_start, key_values, block_lo, block_hi, block_base):
    rows, width = queries.shape
    heads = width // HD
    q_blocks = rows // BQ
    kv_rows = key_values.shape[0]
    grid_spec = pltpu.PrefetchScalarGridSpec(
        num_scalar_prefetch=3,
        grid=(q_blocks, heads),
        in_specs=[
            pl.BlockSpec((BQ, HD), lambda i, h, lo, hi, base: (i, h)),
            pl.BlockSpec((BQ, 1), lambda i, h, lo, hi, base: (i, 0)),
            pl.BlockSpec((kv_rows, 2 * HD), lambda i, h, lo, hi, base: (0, 0)),
        ],
        out_specs=pl.BlockSpec((BQ, HD), lambda i, h, lo, hi, base: (i, h)),
    )
    return pl.pallas_call(
        flash_kernel,
        grid_spec=grid_spec,
        out_shape=jax.ShapeDtypeStruct((rows, width), jnp.bfloat16),
    )(block_lo, block_hi, block_base, queries, row_start, key_values)


def on_device(tokens, norm_gain, w_query, w_key, w_value, w_out, prompt_lengths, page_slots):
    row_count = tokens.shape[0]
    tp_count = lax.axis_size("tpz") * lax.axis_size("tpx")
    seq_rank = lax.axis_index("seq")
    tp_rank = lax.axis_index("tpz") * lax.axis_size("tpx") + lax.axis_index("tpx")
    heads_here = w_query.shape[1] // HD
    kv_heads = w_key.shape[1] // HD
    sharing = tp_count // kv_heads
    kv_head = tp_rank // sharing
    token_index = seq_rank * row_count + jnp.arange(row_count, dtype=jnp.int32)
    start = segment_start(token_index, prompt_lengths)
    position = token_index - start
    normed = normalize(tokens, norm_gain)

    key_columns = lax.dynamic_slice_in_dim(w_key, kv_head * HD, HD, 1)
    value_columns = lax.dynamic_slice_in_dim(w_value, kv_head * HD, HD, 1)
    keys_here = rotate(
        jnp.dot(normed, key_columns, preferred_element_type=jnp.float32)[:, None, :], position
    )[:, 0].astype(jnp.bfloat16)
    values_here = jnp.dot(normed, value_columns, preferred_element_type=jnp.float32).astype(
        jnp.bfloat16
    )
    keys_values = jnp.concatenate([keys_here, values_here], axis=1)
    gathered = lax.all_gather(keys_values, "seq", axis=0, tiled=True)

    queries = rotate(
        jnp.dot(normed, w_query, preferred_element_type=jnp.float32).reshape(
            row_count, heads_here, HD
        ),
        position,
    ).astype(jnp.bfloat16).reshape(row_count, heads_here * HD)

    q_blocks = row_count // BQ
    first_rows = start.reshape(q_blocks, BQ)[:, 0]
    block_base = seq_rank * row_count + BQ * jnp.arange(q_blocks, dtype=jnp.int32)
    block_lo = first_rows // BK
    block_hi = (block_base + BQ - 1) // BK
    heads_out = flash_attention(
        queries, start[:, None], gathered, block_lo, block_hi, block_base
    )

    partial_out = jnp.dot(heads_out, w_out, preferred_element_type=jnp.float32).astype(
        jnp.bfloat16
    )
    partial_out = lax.psum_scatter(partial_out, "tpz", scatter_dimension=0, tiled=True)
    attended = lax.psum_scatter(partial_out, "tpx", scatter_dimension=0, tiled=True)

    cache_width = 2 * HD // sharing
    cache_column = tp_rank % sharing * cache_width
    slots_here = row_count // PAGE
    page_total = page_slots.shape[0]
    wanted = seq_rank * slots_here + jnp.arange(slots_here, dtype=jnp.int32)
    page_of_slot = jnp.sum(
        jnp.where(
            page_slots[None, :] == wanted[:, None],
            jnp.arange(page_total, dtype=jnp.int32)[None, :],
            0,
        ),
        axis=1,
    )
    pages = [
        lax.dynamic_slice(gathered, (page_of_slot[j] * PAGE, cache_column), (PAGE, cache_width))
        for j in range(slots_here)
    ]
    cache_here = jnp.stack(pages, axis=0)
    return (attended, cache_here)


def solution(mesh):
    seq_size, tp_size = mesh.devices.shape
    split_mesh = jax.sharding.Mesh(
        mesh.devices.reshape(seq_size, tp_size // 2, 2), ("seq", "tpz", "tpx")
    )
    tp = ("tpz", "tpx")
    placed = (P("seq", None), P(), P(None, tp), P(), P(), P(tp, None), P(), P())
    return jax.shard_map(
        on_device,
        mesh=split_mesh,
        in_specs=placed,
        out_specs=(P(("seq",) + tp, None), P("seq", None, tp)),
        check_vma=False,
    )
```

```python
import functools

import jax
import jax.numpy as jnp
from jax import lax
from jax.experimental import pallas as pl
from jax.experimental.pallas import tpu as pltpu
from jax.sharding import PartitionSpec as P

HD = 128
PAGE = 128
BQ = 256
BK = 512


epsilon = 1e-05
rope_base = 5000000.0


def segment_start(token_index, prompt_lengths):
    prompt_ends = jnp.cumsum(prompt_lengths)
    finished = prompt_ends[None, :] <= token_index[:, None]
    return jnp.sum(jnp.where(finished, prompt_lengths[None, :], 0), axis=1)


def rotate(vectors, position):
    half_size = HD // 2
    frequency = rope_base ** (-(2.0 * jnp.arange(half_size, dtype=jnp.float32)) / HD)
    angle = position.astype(jnp.float32)[:, None] * frequency[None, :]
    cosine = jnp.cos(angle)[:, None, :]
    sine = jnp.sin(angle)[:, None, :]
    first_half = vectors[..., :half_size]
    second_half = vectors[..., half_size:]
    return jnp.concatenate(
        [first_half * cosine - second_half * sine, second_half * cosine + first_half * sine],
        axis=-1,
    )


def normalize(tokens, norm_gain):
    hidden = tokens.astype(jnp.float32)
    factor = lax.rsqrt(jnp.mean(hidden * hidden, axis=-1, keepdims=True) + epsilon)
    return (hidden * factor * norm_gain.astype(jnp.float32)).astype(jnp.bfloat16)


def flash_kernel(lo_ref, hi_ref, base_ref, last_start_ref, q_ref, start_ref, kt_ref, v_ref, o_ref):
    i = pl.program_id(0)
    q = q_ref[...]
    row_index = base_ref[i] + lax.broadcasted_iota(jnp.int32, (BQ, 1), 0)
    row_start = start_ref[...]
    scale = HD ** (-0.5)

    def step(kb, carry, masked):
        running_max, running_sum, weighted = carry
        offset = pl.multiple_of(kb * BK, BK)
        keys_t = kt_ref[:, pl.ds(offset, BK)]
        values = v_ref[pl.ds(offset, BK), :]
        scores = jnp.dot(q, keys_t, preferred_element_type=jnp.float32) * scale
        if masked:
            key_index = offset + lax.broadcasted_iota(jnp.int32, (1, BK), 1)
            visible = (key_index >= row_start) & (key_index <= row_index)
            scores = jnp.where(visible, scores, -1e30)
        fresh_max = jnp.maximum(running_max, jnp.max(scores, axis=1, keepdims=True))
        weights = jnp.exp(scores - fresh_max)
        if masked:
            weights = jnp.where(visible, weights, 0.0)
        shrink = jnp.exp(running_max - fresh_max)
        running_sum = running_sum * shrink + jnp.sum(weights, axis=1, keepdims=True)
        weighted = weighted * shrink + jnp.dot(
            weights.astype(jnp.bfloat16), values, preferred_element_type=jnp.float32
        )
        return (fresh_max, running_sum, weighted)

    lo = lo_ref[i]
    hi = hi_ref[i] + 1
    full_lo = (last_start_ref[i] + BK - 1) // BK
    full_hi = (base_ref[i] + 1) // BK
    mid_lo = jnp.minimum(jnp.maximum(full_lo, lo), hi)
    mid_hi = jnp.maximum(mid_lo, jnp.minimum(full_hi, hi))
    carry = (
        jnp.full((BQ, 1), -1e30, jnp.float32),
        jnp.zeros((BQ, 1), jnp.float32),
        jnp.zeros((BQ, HD), jnp.float32),
    )
    carry = lax.fori_loop(lo, mid_lo, functools.partial(step, masked=True), carry)
    carry = lax.fori_loop(mid_lo, mid_hi, functools.partial(step, masked=False), carry)
    carry = lax.fori_loop(mid_hi, hi, functools.partial(step, masked=True), carry)
    running_max, running_sum, weighted = carry
    o_ref[...] = (weighted / running_sum).astype(o_ref.dtype)


def flash_attention(queries, row_start, keys_t, values, bounds):
    rows, width = queries.shape
    heads = width // HD
    q_blocks = rows // BQ
    kv_rows = values.shape[0]
    index = lambda i, h, *_: (i, h)
    grid_spec = pltpu.PrefetchScalarGridSpec(
        num_scalar_prefetch=4,
        grid=(q_blocks, heads),
        in_specs=[
            pl.BlockSpec((BQ, HD), index),
            pl.BlockSpec((BQ, 1), lambda i, h, *_: (i, 0)),
            pl.BlockSpec((HD, kv_rows), lambda i, h, *_: (0, 0)),
            pl.BlockSpec((kv_rows, HD), lambda i, h, *_: (0, 0)),
        ],
        out_specs=pl.BlockSpec((BQ, HD), index),
    )
    return pl.pallas_call(
        flash_kernel,
        grid_spec=grid_spec,
        out_shape=jax.ShapeDtypeStruct((rows, width), jnp.bfloat16),
    )(*bounds, queries, row_start, keys_t, values)


def on_device(tokens, norm_gain, w_query, w_key, w_value, w_out, prompt_lengths, page_slots):
    row_count = tokens.shape[0]
    tp_count = lax.axis_size("tpz") * lax.axis_size("tpx")
    seq_rank = lax.axis_index("seq")
    tp_rank = lax.axis_index("tpz") * lax.axis_size("tpx") + lax.axis_index("tpx")
    heads_here = w_query.shape[1] // HD
    kv_heads = w_key.shape[1] // HD
    sharing = tp_count // kv_heads
    kv_head = tp_rank // sharing
    token_index = seq_rank * row_count + jnp.arange(row_count, dtype=jnp.int32)
    start = segment_start(token_index, prompt_lengths)
    position = token_index - start
    normed = normalize(tokens, norm_gain)

    key_columns = lax.dynamic_slice_in_dim(w_key, kv_head * HD, HD, 1)
    value_columns = lax.dynamic_slice_in_dim(w_value, kv_head * HD, HD, 1)
    keys_here = rotate(
        jnp.dot(normed, key_columns, preferred_element_type=jnp.float32)[:, None, :], position
    )[:, 0].astype(jnp.bfloat16)
    values_here = jnp.dot(normed, value_columns, preferred_element_type=jnp.float32).astype(
        jnp.bfloat16
    )
    keys_t = lax.all_gather(keys_here.T, "seq", axis=1, tiled=True)
    values_all = lax.all_gather(values_here, "seq", axis=0, tiled=True)

    queries = rotate(
        jnp.dot(normed, w_query, preferred_element_type=jnp.float32).reshape(
            row_count, heads_here, HD
        ),
        position,
    ).astype(jnp.bfloat16).reshape(row_count, heads_here * HD)

    q_blocks = row_count // BQ
    first_rows = start.reshape(q_blocks, BQ)[:, 0]
    block_base = seq_rank * row_count + BQ * jnp.arange(q_blocks, dtype=jnp.int32)
    last_rows = start.reshape(q_blocks, BQ)[:, -1]
    block_lo = first_rows // BK
    block_hi = (block_base + BQ - 1) // BK
    heads_out = flash_attention(
        queries,
        start[:, None],
        keys_t,
        values_all,
        (block_lo, block_hi, block_base, last_rows),
    )

    partial_out = jnp.dot(heads_out, w_out, preferred_element_type=jnp.float32).astype(
        jnp.bfloat16
    )
    partial_out = lax.psum_scatter(partial_out, "tpz", scatter_dimension=0, tiled=True)
    attended = lax.psum_scatter(partial_out, "tpx", scatter_dimension=0, tiled=True)

    slots_here = row_count // PAGE
    page_total = page_slots.shape[0]
    wanted = seq_rank * slots_here + jnp.arange(slots_here, dtype=jnp.int32)
    page_of_slot = jnp.sum(
        jnp.where(
            page_slots[None, :] == wanted[:, None],
            jnp.arange(page_total, dtype=jnp.int32)[None, :],
            0,
        ),
        axis=1,
    )
    key_pages = jnp.stack(
        [lax.dynamic_slice_in_dim(keys_t, page_of_slot[j] * PAGE, PAGE, 1).T for j in range(slots_here)]
    )
    value_pages = jnp.stack(
        [lax.dynamic_slice_in_dim(values_all, page_of_slot[j] * PAGE, PAGE, 0) for j in range(slots_here)]
    )
    cache_here = jnp.where(tp_rank % sharing == 0, key_pages, value_pages)
    return (attended, cache_here)


def solution(mesh):
    seq_size, tp_size = mesh.devices.shape
    split_mesh = jax.sharding.Mesh(
        mesh.devices.reshape(seq_size, tp_size // 2, 2), ("seq", "tpz", "tpx")
    )
    tp = ("tpz", "tpx")
    placed = (P("seq", None), P(), P(None, tp), P(), P(), P(tp, None), P(), P())
    return jax.shard_map(
        on_device,
        mesh=split_mesh,
        in_specs=placed,
        out_specs=(P(("seq",) + tp, None), P("seq", None, tp)),
        check_vma=False,
    )
```

```python
import functools

import jax
import jax.numpy as jnp
from jax import lax
from jax.experimental import pallas as pl
from jax.experimental.pallas import tpu as pltpu
from jax.sharding import PartitionSpec as P

HD = 128
PAGE = 128
BQ = 128
CHUNKS = 4
BK = 512


epsilon = 1e-05
rope_base = 5000000.0


def segment_start(token_index, prompt_lengths):
    prompt_ends = jnp.cumsum(prompt_lengths)
    finished = prompt_ends[None, :] <= token_index[:, None]
    return jnp.sum(jnp.where(finished, prompt_lengths[None, :], 0), axis=1)


def rotate(vectors, position):
    half_size = HD // 2
    frequency = rope_base ** (-(2.0 * jnp.arange(half_size, dtype=jnp.float32)) / HD)
    angle = position.astype(jnp.float32)[:, None] * frequency[None, :]
    cosine = jnp.cos(angle)[:, None, :]
    sine = jnp.sin(angle)[:, None, :]
    first_half = vectors[..., :half_size]
    second_half = vectors[..., half_size:]
    return jnp.concatenate(
        [first_half * cosine - second_half * sine, second_half * cosine + first_half * sine],
        axis=-1,
    )


def normalize(tokens, norm_gain):
    hidden = tokens.astype(jnp.float32)
    factor = lax.rsqrt(jnp.mean(hidden * hidden, axis=-1, keepdims=True) + epsilon)
    return (hidden * factor * norm_gain.astype(jnp.float32)).astype(jnp.bfloat16)


def flash_kernel(lo_ref, hi_ref, base_ref, last_start_ref, q_ref, start_ref, index_ref, kt_ref, kv_ref, o_ref):
    i = pl.program_id(0)
    q = q_ref[...]
    row_index = index_ref[...]
    row_start = start_ref[...]
    scale = HD ** (-0.5)

    def step(kb, carry, masked):
        running_max, running_sum, weighted = carry
        offset = pl.multiple_of(kb * BK, BK)
        keys_t = kt_ref[:, pl.ds(offset, BK)]
        values = kv_ref[pl.ds(offset, BK), pl.ds(HD, HD)]
        scores = jnp.dot(q, keys_t, preferred_element_type=jnp.float32) * scale
        if masked:
            key_index = offset + lax.broadcasted_iota(jnp.int32, (1, BK), 1)
            visible = (key_index >= row_start) & (key_index <= row_index)
            scores = jnp.where(visible, scores, -1e30)
        fresh_max = jnp.maximum(running_max, jnp.max(scores, axis=1, keepdims=True))
        weights = jnp.exp(scores - fresh_max)
        if masked:
            weights = jnp.where(visible, weights, 0.0)
        shrink = jnp.exp(running_max - fresh_max)
        running_sum = running_sum * shrink + jnp.sum(weights, axis=1, keepdims=True)
        weighted = weighted * shrink + jnp.dot(
            weights.astype(jnp.bfloat16), values, preferred_element_type=jnp.float32
        )
        return (fresh_max, running_sum, weighted)

    lo = lo_ref[i]
    hi = hi_ref[i] + 1
    full_lo = (last_start_ref[i] + BK - 1) // BK
    full_hi = (base_ref[i] + 1) // BK
    mid_lo = jnp.minimum(jnp.maximum(full_lo, lo), hi)
    mid_hi = jnp.maximum(mid_lo, jnp.minimum(full_hi, hi))
    carry = (
        jnp.full((BQ, 1), -1e30, jnp.float32),
        jnp.zeros((BQ, 1), jnp.float32),
        jnp.zeros((BQ, HD), jnp.float32),
    )
    carry = lax.fori_loop(lo, mid_lo, functools.partial(step, masked=True), carry)
    carry = lax.fori_loop(mid_lo, mid_hi, functools.partial(step, masked=False), carry)
    carry = lax.fori_loop(mid_hi, hi, functools.partial(step, masked=True), carry)
    running_max, running_sum, weighted = carry
    o_ref[...] = (weighted / running_sum).astype(o_ref.dtype)


def flash_attention(queries, row_start, row_index, keys_t, key_values, bounds):
    rows, width = queries.shape
    heads = width // HD
    q_blocks = rows // BQ
    kv_rows = key_values.shape[0]
    index = lambda i, h, *_: (i, h)
    rows_of = lambda i, h, *_: (i, 0)
    grid_spec = pltpu.PrefetchScalarGridSpec(
        num_scalar_prefetch=4,
        grid=(q_blocks, heads),
        in_specs=[
            pl.BlockSpec((BQ, HD), index),
            pl.BlockSpec((BQ, 1), rows_of),
            pl.BlockSpec((BQ, 1), rows_of),
            pl.BlockSpec((HD, kv_rows), lambda i, h, *_: (0, 0)),
            pl.BlockSpec((kv_rows, 2 * HD), lambda i, h, *_: (0, 0)),
        ],
        out_specs=pl.BlockSpec((BQ, HD), index),
    )
    return pl.pallas_call(
        flash_kernel,
        grid_spec=grid_spec,
        out_shape=jax.ShapeDtypeStruct((rows, width), jnp.bfloat16),
    )(*bounds, queries, row_start, row_index, keys_t, key_values)


def on_device(tokens, norm_gain, w_query, w_key, w_value, w_out, prompt_lengths, page_slots):
    row_count = tokens.shape[0]
    tp_count = lax.axis_size("tpz") * lax.axis_size("tpx")
    seq_rank = lax.axis_index("seq")
    tp_rank = lax.axis_index("tpz") * lax.axis_size("tpx") + lax.axis_index("tpx")
    heads_here = w_query.shape[1] // HD
    kv_heads = w_key.shape[1] // HD
    sharing = tp_count // kv_heads
    kv_head = tp_rank // sharing
    token_index = seq_rank * row_count + jnp.arange(row_count, dtype=jnp.int32)
    start = segment_start(token_index, prompt_lengths)
    position = token_index - start
    normed = normalize(tokens, norm_gain)

    key_columns = lax.dynamic_slice_in_dim(w_key, kv_head * HD, HD, 1)
    value_columns = lax.dynamic_slice_in_dim(w_value, kv_head * HD, HD, 1)
    keys_here = rotate(
        jnp.dot(normed, key_columns, preferred_element_type=jnp.float32)[:, None, :], position
    )[:, 0].astype(jnp.bfloat16)
    values_here = jnp.dot(normed, value_columns, preferred_element_type=jnp.float32).astype(
        jnp.bfloat16
    )
    keys_values = jnp.concatenate([keys_here, values_here], axis=1)
    gathered = lax.all_gather(keys_values, "seq", axis=0, tiled=True)
    keys_t = gathered[:, :HD].T

    queries = rotate(
        jnp.dot(normed, w_query, preferred_element_type=jnp.float32).reshape(
            row_count, heads_here, HD
        ),
        position,
    ).astype(jnp.bfloat16).reshape(row_count, heads_here * HD)

    piece = row_count // tp_count // CHUNKS
    chunk_queries = queries.reshape(tp_count, CHUNKS, piece, heads_here * HD)
    chunk_start = start.reshape(tp_count, CHUNKS, piece)
    chunk_index = token_index.reshape(tp_count, CHUNKS, piece)
    outputs = []
    for c in range(CHUNKS):
        q_rows = chunk_queries[:, c].reshape(tp_count * piece, heads_here * HD)
        s_rows = chunk_start[:, c].reshape(tp_count * piece)
        i_rows = chunk_index[:, c].reshape(tp_count * piece)
        bounds = (s_rows[:1] // BK, i_rows[-1:] // BK, i_rows[:1], s_rows[-1:])
        heads_out = flash_attention(
            q_rows, s_rows[:, None], i_rows[:, None], keys_t, gathered, bounds
        )
        partial_out = jnp.dot(heads_out, w_out, preferred_element_type=jnp.float32).astype(
            jnp.bfloat16
        )
        partial_out = lax.psum_scatter(partial_out, "tpz", scatter_dimension=0, tiled=True)
        outputs.append(lax.psum_scatter(partial_out, "tpx", scatter_dimension=0, tiled=True))
    attended = jnp.stack(outputs, axis=0).reshape(-1, outputs[0].shape[1])

    cache_width = 2 * HD // sharing
    cache_column = tp_rank % sharing * cache_width
    slots_here = row_count // PAGE
    page_total = page_slots.shape[0]
    wanted = seq_rank * slots_here + jnp.arange(slots_here, dtype=jnp.int32)
    page_of_slot = jnp.sum(
        jnp.where(
            page_slots[None, :] == wanted[:, None],
            jnp.arange(page_total, dtype=jnp.int32)[None, :],
            0,
        ),
        axis=1,
    )
    pages = [
        lax.dynamic_slice(gathered, (page_of_slot[j] * PAGE, cache_column), (PAGE, cache_width))
        for j in range(slots_here)
    ]
    cache_here = jnp.stack(pages, axis=0)
    return (attended, cache_here)


def solution(mesh):
    seq_size, tp_size = mesh.devices.shape
    split_mesh = jax.sharding.Mesh(
        mesh.devices.reshape(seq_size, tp_size // 2, 2), ("seq", "tpz", "tpx")
    )
    tp = ("tpz", "tpx")
    placed = (P("seq", None), P(), P(None, tp), P(), P(), P(tp, None), P(), P())
    return jax.shard_map(
        on_device,
        mesh=split_mesh,
        in_specs=placed,
        out_specs=(P(("seq",) + tp, None), P("seq", None, tp)),
        check_vma=False,
    )
```

```python
import functools

import jax
import jax.numpy as jnp
from jax import lax
from jax.experimental import pallas as pl
from jax.experimental.pallas import tpu as pltpu
from jax.sharding import PartitionSpec as P

HD = 128
PAGE = 128
BQ = 256
BK = 512


epsilon = 1e-05
rope_base = 5000000.0


def segment_start(token_index, prompt_lengths):
    prompt_ends = jnp.cumsum(prompt_lengths)
    finished = prompt_ends[None, :] <= token_index[:, None]
    return jnp.sum(jnp.where(finished, prompt_lengths[None, :], 0), axis=1)


def rotate(vectors, position):
    half_size = HD // 2
    frequency = rope_base ** (-(2.0 * jnp.arange(half_size, dtype=jnp.float32)) / HD)
    angle = position.astype(jnp.float32)[:, None] * frequency[None, :]
    cosine = jnp.cos(angle)[:, None, :]
    sine = jnp.sin(angle)[:, None, :]
    first_half = vectors[..., :half_size]
    second_half = vectors[..., half_size:]
    return jnp.concatenate(
        [first_half * cosine - second_half * sine, second_half * cosine + first_half * sine],
        axis=-1,
    )


def normalize(tokens, norm_gain):
    hidden = tokens.astype(jnp.float32)
    factor = lax.rsqrt(jnp.mean(hidden * hidden, axis=-1, keepdims=True) + epsilon)
    return (hidden * factor * norm_gain.astype(jnp.float32)).astype(jnp.bfloat16)


def flash_kernel(lo_ref, hi_ref, base_ref, last_start_ref, q_ref, start_ref, kt_ref, kv_ref, o_ref):
    i = pl.program_id(0)
    q = q_ref[...]
    row_index = base_ref[i] + lax.broadcasted_iota(jnp.int32, (BQ, 1), 0)
    row_start = start_ref[...]
    scale = HD ** (-0.5)

    def step(kb, carry, masked):
        running_max, running_sum, weighted = carry
        offset = pl.multiple_of(kb * BK, BK)
        keys_t = kt_ref[:, pl.ds(offset, BK)]
        values = kv_ref[pl.ds(offset, BK), pl.ds(HD, HD)]
        scores = jnp.dot(q, keys_t, preferred_element_type=jnp.float32) * scale
        if masked:
            key_index = offset + lax.broadcasted_iota(jnp.int32, (1, BK), 1)
            visible = (key_index >= row_start) & (key_index <= row_index)
            scores = jnp.where(visible, scores, -1e30)
        fresh_max = jnp.maximum(running_max, jnp.max(scores, axis=1, keepdims=True))
        weights = jnp.exp(scores - fresh_max)
        if masked:
            weights = jnp.where(visible, weights, 0.0)
        shrink = jnp.exp(running_max - fresh_max)
        running_sum = running_sum * shrink + jnp.sum(weights, axis=1, keepdims=True)
        weighted = weighted * shrink + jnp.dot(
            weights.astype(jnp.bfloat16), values, preferred_element_type=jnp.float32
        )
        return (fresh_max, running_sum, weighted)

    lo = lo_ref[i]
    hi = hi_ref[i] + 1
    full_lo = (last_start_ref[i] + BK - 1) // BK
    full_hi = (base_ref[i] + 1) // BK
    mid_lo = jnp.minimum(jnp.maximum(full_lo, lo), hi)
    mid_hi = jnp.maximum(mid_lo, jnp.minimum(full_hi, hi))
    carry = (
        jnp.full((BQ, 1), -1e30, jnp.float32),
        jnp.zeros((BQ, 1), jnp.float32),
        jnp.zeros((BQ, HD), jnp.float32),
    )
    carry = lax.fori_loop(lo, mid_lo, functools.partial(step, masked=True), carry)
    carry = lax.fori_loop(mid_lo, mid_hi, functools.partial(step, masked=False), carry)
    carry = lax.fori_loop(mid_hi, hi, functools.partial(step, masked=True), carry)
    running_max, running_sum, weighted = carry
    o_ref[...] = (weighted / running_sum).astype(o_ref.dtype)


def flash_attention(queries, row_start, keys_t, values, bounds):
    rows, width = queries.shape
    heads = width // HD
    q_blocks = rows // BQ
    kv_rows = values.shape[0]
    index = lambda i, h, *_: (i, h)
    grid_spec = pltpu.PrefetchScalarGridSpec(
        num_scalar_prefetch=4,
        grid=(q_blocks, heads),
        in_specs=[
            pl.BlockSpec((BQ, HD), index),
            pl.BlockSpec((BQ, 1), lambda i, h, *_: (i, 0)),
            pl.BlockSpec((HD, kv_rows), lambda i, h, *_: (0, 0)),
            pl.BlockSpec((kv_rows, 2 * HD), lambda i, h, *_: (0, 0)),
        ],
        out_specs=pl.BlockSpec((BQ, HD), index),
    )
    return pl.pallas_call(
        flash_kernel,
        grid_spec=grid_spec,
        out_shape=jax.ShapeDtypeStruct((rows, width), jnp.bfloat16),
    )(*bounds, queries, row_start, keys_t, values)


def on_device(tokens, norm_gain, w_query, w_key, w_value, w_out, prompt_lengths, page_slots):
    row_count = tokens.shape[0]
    tp_count = lax.axis_size("tpz") * lax.axis_size("tpx")
    seq_rank = lax.axis_index("seq")
    tp_rank = lax.axis_index("tpz") * lax.axis_size("tpx") + lax.axis_index("tpx")
    heads_here = w_query.shape[1] // HD
    kv_heads = w_key.shape[1] // HD
    sharing = tp_count // kv_heads
    kv_head = tp_rank // sharing
    token_index = seq_rank * row_count + jnp.arange(row_count, dtype=jnp.int32)
    start = segment_start(token_index, prompt_lengths)
    position = token_index - start
    normed = normalize(tokens, norm_gain)

    key_columns = lax.dynamic_slice_in_dim(w_key, kv_head * HD, HD, 1)
    value_columns = lax.dynamic_slice_in_dim(w_value, kv_head * HD, HD, 1)
    keys_here = rotate(
        jnp.dot(normed, key_columns, preferred_element_type=jnp.float32)[:, None, :], position
    )[:, 0].astype(jnp.bfloat16)
    values_here = jnp.dot(normed, value_columns, preferred_element_type=jnp.float32).astype(
        jnp.bfloat16
    )
    keys_values = jnp.concatenate([keys_here, values_here], axis=1)
    gathered = lax.all_gather(keys_values, "seq", axis=0, tiled=True)
    keys_t = gathered[:, :HD].T

    queries = rotate(
        jnp.dot(normed, w_query, preferred_element_type=jnp.float32).reshape(
            row_count, heads_here, HD
        ),
        position,
    ).astype(jnp.bfloat16).reshape(row_count, heads_here * HD)

    q_blocks = row_count // BQ
    first_rows = start.reshape(q_blocks, BQ)[:, 0]
    block_base = seq_rank * row_count + BQ * jnp.arange(q_blocks, dtype=jnp.int32)
    last_rows = start.reshape(q_blocks, BQ)[:, -1]
    block_lo = first_rows // BK
    block_hi = (block_base + BQ - 1) // BK
    heads_out = flash_attention(
        queries,
        start[:, None],
        keys_t,
        gathered,
        (block_lo, block_hi, block_base, last_rows),
    )

    partial_out = jnp.dot(heads_out, w_out, preferred_element_type=jnp.float32).astype(
        jnp.bfloat16
    )
    received = lax.all_to_all(
        partial_out, ("tpz", "tpx"), split_axis=0, concat_axis=0, tiled=True
    )
    received = received.reshape(tp_count, row_count // tp_count, -1)
    summed = received[0].astype(jnp.float32)
    for t in range(1, tp_count):
        summed = summed + received[t].astype(jnp.float32)
    attended = summed.astype(jnp.bfloat16)

    cache_width = 2 * HD // sharing
    cache_column = tp_rank % sharing * cache_width
    slots_here = row_count // PAGE
    page_total = page_slots.shape[0]
    wanted = seq_rank * slots_here + jnp.arange(slots_here, dtype=jnp.int32)
    page_of_slot = jnp.sum(
        jnp.where(
            page_slots[None, :] == wanted[:, None],
            jnp.arange(page_total, dtype=jnp.int32)[None, :],
            0,
        ),
        axis=1,
    )
    pages = [
        lax.dynamic_slice(gathered, (page_of_slot[j] * PAGE, cache_column), (PAGE, cache_width))
        for j in range(slots_here)
    ]
    cache_here = jnp.stack(pages, axis=0)
    return (attended, cache_here)


def solution(mesh):
    seq_size, tp_size = mesh.devices.shape
    split_mesh = jax.sharding.Mesh(
        mesh.devices.reshape(seq_size, tp_size // 2, 2), ("seq", "tpz", "tpx")
    )
    tp = ("tpz", "tpx")
    placed = (P("seq", None), P(), P(None, tp), P(), P(), P(tp, None), P(), P())
    return jax.shard_map(
        on_device,
        mesh=split_mesh,
        in_specs=placed,
        out_specs=(P(("seq",) + tp, None), P("seq", None, tp)),
        check_vma=False,
    )
```

```python
import functools

import jax
import jax.numpy as jnp
from jax import lax
from jax.experimental import pallas as pl
from jax.experimental.pallas import tpu as pltpu
from jax.sharding import PartitionSpec as P

HD = 128
PAGE = 128
BQ = 256
CHUNKS = 2
BK = 512


epsilon = 1e-05
rope_base = 5000000.0


def segment_start(token_index, prompt_lengths):
    prompt_ends = jnp.cumsum(prompt_lengths)
    finished = prompt_ends[None, :] <= token_index[:, None]
    return jnp.sum(jnp.where(finished, prompt_lengths[None, :], 0), axis=1)


def rotate(vectors, position):
    half_size = HD // 2
    frequency = rope_base ** (-(2.0 * jnp.arange(half_size, dtype=jnp.float32)) / HD)
    angle = position.astype(jnp.float32)[:, None] * frequency[None, :]
    cosine = jnp.cos(angle)[:, None, :]
    sine = jnp.sin(angle)[:, None, :]
    first_half = vectors[..., :half_size]
    second_half = vectors[..., half_size:]
    return jnp.concatenate(
        [first_half * cosine - second_half * sine, second_half * cosine + first_half * sine],
        axis=-1,
    )


def normalize(tokens, norm_gain):
    hidden = tokens.astype(jnp.float32)
    factor = lax.rsqrt(jnp.mean(hidden * hidden, axis=-1, keepdims=True) + epsilon)
    return (hidden * factor * norm_gain.astype(jnp.float32)).astype(jnp.bfloat16)


def flash_kernel(lo_ref, hi_ref, base_ref, last_start_ref, q_ref, start_ref, index_ref, kt_ref, kv_ref, o_ref):
    i = pl.program_id(0)
    q = q_ref[...]
    row_index = index_ref[...]
    row_start = start_ref[...]
    scale = HD ** (-0.5)

    def step(kb, carry, masked):
        running_max, running_sum, weighted = carry
        offset = pl.multiple_of(kb * BK, BK)
        keys_t = kt_ref[:, pl.ds(offset, BK)]
        values = kv_ref[pl.ds(offset, BK), pl.ds(HD, HD)]
        scores = jnp.dot(q, keys_t, preferred_element_type=jnp.float32) * scale
        if masked:
            key_index = offset + lax.broadcasted_iota(jnp.int32, (1, BK), 1)
            visible = (key_index >= row_start) & (key_index <= row_index)
            scores = jnp.where(visible, scores, -1e30)
        fresh_max = jnp.maximum(running_max, jnp.max(scores, axis=1, keepdims=True))
        weights = jnp.exp(scores - fresh_max)
        if masked:
            weights = jnp.where(visible, weights, 0.0)
        shrink = jnp.exp(running_max - fresh_max)
        running_sum = running_sum * shrink + jnp.sum(weights, axis=1, keepdims=True)
        weighted = weighted * shrink + jnp.dot(
            weights.astype(jnp.bfloat16), values, preferred_element_type=jnp.float32
        )
        return (fresh_max, running_sum, weighted)

    lo = lo_ref[i]
    hi = hi_ref[i] + 1
    full_lo = (last_start_ref[i] + BK - 1) // BK
    full_hi = (base_ref[i] + 1) // BK
    mid_lo = jnp.minimum(jnp.maximum(full_lo, lo), hi)
    mid_hi = jnp.maximum(mid_lo, jnp.minimum(full_hi, hi))
    carry = (
        jnp.full((BQ, 1), -1e30, jnp.float32),
        jnp.zeros((BQ, 1), jnp.float32),
        jnp.zeros((BQ, HD), jnp.float32),
    )
    carry = lax.fori_loop(lo, mid_lo, functools.partial(step, masked=True), carry)
    carry = lax.fori_loop(mid_lo, mid_hi, functools.partial(step, masked=False), carry)
    carry = lax.fori_loop(mid_hi, hi, functools.partial(step, masked=True), carry)
    running_max, running_sum, weighted = carry
    o_ref[...] = (weighted / running_sum).astype(o_ref.dtype)


def flash_attention(queries, row_start, row_index, keys_t, key_values, bounds):
    rows, width = queries.shape
    heads = width // HD
    q_blocks = rows // BQ
    kv_rows = key_values.shape[0]
    index = lambda i, h, *_: (i, h)
    rows_of = lambda i, h, *_: (i, 0)
    grid_spec = pltpu.PrefetchScalarGridSpec(
        num_scalar_prefetch=4,
        grid=(q_blocks, heads),
        in_specs=[
            pl.BlockSpec((BQ, HD), index),
            pl.BlockSpec((BQ, 1), rows_of),
            pl.BlockSpec((BQ, 1), rows_of),
            pl.BlockSpec((HD, kv_rows), lambda i, h, *_: (0, 0)),
            pl.BlockSpec((kv_rows, 2 * HD), lambda i, h, *_: (0, 0)),
        ],
        out_specs=pl.BlockSpec((BQ, HD), index),
    )
    return pl.pallas_call(
        flash_kernel,
        grid_spec=grid_spec,
        out_shape=jax.ShapeDtypeStruct((rows, width), jnp.bfloat16),
    )(*bounds, queries, row_start, row_index, keys_t, key_values)


def on_device(tokens, norm_gain, w_query, w_key, w_value, w_out, prompt_lengths, page_slots):
    row_count = tokens.shape[0]
    tp_count = lax.axis_size("tpz") * lax.axis_size("tpx")
    seq_rank = lax.axis_index("seq")
    tp_rank = lax.axis_index("tpz") * lax.axis_size("tpx") + lax.axis_index("tpx")
    heads_here = w_query.shape[1] // HD
    kv_heads = w_key.shape[1] // HD
    sharing = tp_count // kv_heads
    kv_head = tp_rank // sharing
    token_index = seq_rank * row_count + jnp.arange(row_count, dtype=jnp.int32)
    start = segment_start(token_index, prompt_lengths)
    position = token_index - start
    normed = normalize(tokens, norm_gain)

    key_columns = lax.dynamic_slice_in_dim(w_key, kv_head * HD, HD, 1)
    value_columns = lax.dynamic_slice_in_dim(w_value, kv_head * HD, HD, 1)
    keys_here = rotate(
        jnp.dot(normed, key_columns, preferred_element_type=jnp.float32)[:, None, :], position
    )[:, 0].astype(jnp.bfloat16)
    values_here = jnp.dot(normed, value_columns, preferred_element_type=jnp.float32).astype(
        jnp.bfloat16
    )
    keys_values = jnp.concatenate([keys_here, values_here], axis=1)
    gathered = lax.all_gather(keys_values, "seq", axis=0, tiled=True)
    keys_t = gathered[:, :HD].T

    queries = rotate(
        jnp.dot(normed, w_query, preferred_element_type=jnp.float32).reshape(
            row_count, heads_here, HD
        ),
        position,
    ).astype(jnp.bfloat16).reshape(row_count, heads_here * HD)

    piece = row_count // tp_count // CHUNKS
    chunk_queries = queries.reshape(tp_count, CHUNKS, piece, heads_here * HD)
    chunk_start = start.reshape(tp_count, CHUNKS, piece)
    chunk_index = token_index.reshape(tp_count, CHUNKS, piece)
    outputs = []
    for c in range(CHUNKS):
        q_rows = chunk_queries[:, c].reshape(tp_count * piece, heads_here * HD)
        s_rows = chunk_start[:, c].reshape(tp_count * piece)
        i_rows = chunk_index[:, c].reshape(tp_count * piece)
        bounds = (s_rows[:1] // BK, i_rows[-1:] // BK, i_rows[:1], s_rows[-1:])
        heads_out = flash_attention(
            q_rows, s_rows[:, None], i_rows[:, None], keys_t, gathered, bounds
        )
        partial_out = jnp.dot(heads_out, w_out, preferred_element_type=jnp.float32).astype(
            jnp.bfloat16
        )
        received = lax.all_to_all(
            partial_out, ("tpz", "tpx"), split_axis=0, concat_axis=0, tiled=True
        ).reshape(tp_count, piece, -1)
        summed = received[0].astype(jnp.float32)
        for t in range(1, tp_count):
            summed = summed + received[t].astype(jnp.float32)
        outputs.append(summed.astype(jnp.bfloat16))
    attended = jnp.stack(outputs, axis=0).reshape(-1, outputs[0].shape[1])

    cache_width = 2 * HD // sharing
    cache_column = tp_rank % sharing * cache_width
    slots_here = row_count // PAGE
    page_total = page_slots.shape[0]
    wanted = seq_rank * slots_here + jnp.arange(slots_here, dtype=jnp.int32)
    page_of_slot = jnp.sum(
        jnp.where(
            page_slots[None, :] == wanted[:, None],
            jnp.arange(page_total, dtype=jnp.int32)[None, :],
            0,
        ),
        axis=1,
    )
    pages = [
        lax.dynamic_slice(gathered, (page_of_slot[j] * PAGE, cache_column), (PAGE, cache_width))
        for j in range(slots_here)
    ]
    cache_here = jnp.stack(pages, axis=0)
    return (attended, cache_here)


def solution(mesh):
    seq_size, tp_size = mesh.devices.shape
    split_mesh = jax.sharding.Mesh(
        mesh.devices.reshape(seq_size, tp_size // 2, 2), ("seq", "tpz", "tpx")
    )
    tp = ("tpz", "tpx")
    placed = (P("seq", None), P(), P(None, tp), P(), P(), P(tp, None), P(), P())
    return jax.shard_map(
        on_device,
        mesh=split_mesh,
        in_specs=placed,
        out_specs=(P(("seq",) + tp, None), P("seq", None, tp)),
        check_vma=False,
    )
```

```python
import functools

import jax
import jax.numpy as jnp
from jax import lax
from jax.experimental import pallas as pl
from jax.experimental.pallas import tpu as pltpu
from jax.sharding import PartitionSpec as P

HD = 128
PAGE = 128
BQ = 256
CHUNKS = 2
BK = 1024


epsilon = 1e-05
rope_base = 5000000.0


def segment_start(token_index, prompt_lengths):
    prompt_ends = jnp.cumsum(prompt_lengths)
    finished = prompt_ends[None, :] <= token_index[:, None]
    return jnp.sum(jnp.where(finished, prompt_lengths[None, :], 0), axis=1)


def rotate(vectors, position):
    half_size = HD // 2
    frequency = rope_base ** (-(2.0 * jnp.arange(half_size, dtype=jnp.float32)) / HD)
    angle = position.astype(jnp.float32)[:, None] * frequency[None, :]
    cosine = jnp.cos(angle)[:, None, :]
    sine = jnp.sin(angle)[:, None, :]
    first_half = vectors[..., :half_size]
    second_half = vectors[..., half_size:]
    return jnp.concatenate(
        [first_half * cosine - second_half * sine, second_half * cosine + first_half * sine],
        axis=-1,
    )


def normalize(tokens, norm_gain):
    hidden = tokens.astype(jnp.float32)
    factor = lax.rsqrt(jnp.mean(hidden * hidden, axis=-1, keepdims=True) + epsilon)
    return (hidden * factor * norm_gain.astype(jnp.float32)).astype(jnp.bfloat16)


def flash_kernel(lo_ref, hi_ref, base_ref, last_start_ref, q_ref, start_ref, index_ref, kv_ref, o_ref):
    i = pl.program_id(0)
    heads = q_ref.shape[1] // HD
    row_index = index_ref[...]
    row_start = start_ref[...]
    scale = HD ** (-0.5)

    def step(kb, carry, masked):
        offset = pl.multiple_of(kb * BK, BK)
        keys = kv_ref[pl.ds(offset, BK), pl.ds(0, HD)]
        values = kv_ref[pl.ds(offset, BK), pl.ds(HD, HD)]
        if masked:
            key_index = offset + lax.broadcasted_iota(jnp.int32, (1, BK), 1)
            visible = (key_index >= row_start) & (key_index <= row_index)
        updated = []
        for h in range(heads):
            running_max, running_sum, weighted = carry[h]
            q = q_ref[:, pl.ds(h * HD, HD)]
            scores = lax.dot_general(
                q, keys, (((1,), (1,)), ((), ())), preferred_element_type=jnp.float32
            ) * scale
            if masked:
                scores = jnp.where(visible, scores, -1e30)
            fresh_max = jnp.maximum(running_max, jnp.max(scores, axis=1, keepdims=True))
            weights = jnp.exp(scores - fresh_max)
            if masked:
                weights = jnp.where(visible, weights, 0.0)
            shrink = jnp.exp(running_max - fresh_max)
            running_sum = running_sum * shrink + jnp.sum(weights, axis=1, keepdims=True)
            weighted = weighted * shrink + jnp.dot(
                weights.astype(jnp.bfloat16), values, preferred_element_type=jnp.float32
            )
            updated.append((fresh_max, running_sum, weighted))
        return tuple(updated)

    lo = lo_ref[i]
    hi = hi_ref[i] + 1
    full_lo = (last_start_ref[i] + BK - 1) // BK
    full_hi = (base_ref[i] + 1) // BK
    mid_lo = jnp.minimum(jnp.maximum(full_lo, lo), hi)
    mid_hi = jnp.maximum(mid_lo, jnp.minimum(full_hi, hi))
    carry = tuple(
        (
            jnp.full((BQ, 1), -1e30, jnp.float32),
            jnp.zeros((BQ, 1), jnp.float32),
            jnp.zeros((BQ, HD), jnp.float32),
        )
        for h in range(heads)
    )
    before = mid_lo - lo

    def masked_step(j, carry):
        kb = jnp.where(j < before, lo + j, mid_hi + j - before)
        return step(kb, carry, masked=True)

    carry = lax.fori_loop(0, before + hi - mid_hi, masked_step, carry)
    carry = lax.fori_loop(mid_lo, mid_hi, functools.partial(step, masked=False), carry)
    for h in range(heads):
        running_max, running_sum, weighted = carry[h]
        o_ref[:, pl.ds(h * HD, HD)] = (weighted / running_sum).astype(o_ref.dtype)


def flash_attention(queries, row_start, row_index, key_values, bounds):
    rows, width = queries.shape
    q_blocks = rows // BQ
    kv_rows = key_values.shape[0]
    rows_of = lambda i, *_: (i, 0)
    grid_spec = pltpu.PrefetchScalarGridSpec(
        num_scalar_prefetch=4,
        grid=(q_blocks,),
        in_specs=[
            pl.BlockSpec((BQ, width), rows_of),
            pl.BlockSpec((BQ, 1), rows_of),
            pl.BlockSpec((BQ, 1), rows_of),
            pl.BlockSpec((kv_rows, 2 * HD), lambda i, *_: (0, 0)),
        ],
        out_specs=pl.BlockSpec((BQ, width), rows_of),
    )
    return pl.pallas_call(
        flash_kernel,
        grid_spec=grid_spec,
        out_shape=jax.ShapeDtypeStruct((rows, width), jnp.bfloat16),
    )(*bounds, queries, row_start, row_index, key_values)


def on_device(tokens, norm_gain, w_query, w_key, w_value, w_out, prompt_lengths, page_slots):
    row_count = tokens.shape[0]
    tp_count = lax.axis_size("tpz") * lax.axis_size("tpx")
    seq_rank = lax.axis_index("seq")
    tp_rank = lax.axis_index("tpz") * lax.axis_size("tpx") + lax.axis_index("tpx")
    heads_here = w_query.shape[1] // HD
    kv_heads = w_key.shape[1] // HD
    sharing = tp_count // kv_heads
    kv_head = tp_rank // sharing
    token_index = seq_rank * row_count + jnp.arange(row_count, dtype=jnp.int32)
    start = segment_start(token_index, prompt_lengths)
    position = token_index - start
    normed = normalize(tokens, norm_gain)

    key_columns = lax.dynamic_slice_in_dim(w_key, kv_head * HD, HD, 1)
    value_columns = lax.dynamic_slice_in_dim(w_value, kv_head * HD, HD, 1)
    keys_here = rotate(
        jnp.dot(normed, key_columns, preferred_element_type=jnp.float32)[:, None, :], position
    )[:, 0].astype(jnp.bfloat16)
    values_here = jnp.dot(normed, value_columns, preferred_element_type=jnp.float32).astype(
        jnp.bfloat16
    )
    keys_values = jnp.concatenate([keys_here, values_here], axis=1)
    gathered = lax.all_gather(keys_values, "seq", axis=0, tiled=True)

    queries = rotate(
        jnp.dot(normed, w_query, preferred_element_type=jnp.float32).reshape(
            row_count, heads_here, HD
        ),
        position,
    ).astype(jnp.bfloat16).reshape(row_count, heads_here * HD)

    piece = row_count // tp_count // CHUNKS
    chunk_queries = queries.reshape(tp_count, CHUNKS, piece, heads_here * HD)
    chunk_start = start.reshape(tp_count, CHUNKS, piece)
    chunk_index = token_index.reshape(tp_count, CHUNKS, piece)
    outputs = []
    for c in range(CHUNKS):
        q_rows = chunk_queries[:, c].reshape(tp_count * piece, heads_here * HD)
        s_rows = chunk_start[:, c].reshape(tp_count * piece)
        i_rows = chunk_index[:, c].reshape(tp_count * piece)
        bounds = (s_rows[:1] // BK, i_rows[-1:] // BK, i_rows[:1], s_rows[-1:])
        heads_out = flash_attention(
            q_rows, s_rows[:, None], i_rows[:, None], gathered, bounds
        )
        partial_out = jnp.dot(heads_out, w_out, preferred_element_type=jnp.float32).astype(
            jnp.bfloat16
        )
        received = lax.all_to_all(
            partial_out, ("tpz", "tpx"), split_axis=0, concat_axis=0, tiled=True
        ).reshape(tp_count, piece, -1)
        summed = received[0].astype(jnp.float32)
        for t in range(1, tp_count):
            summed = summed + received[t].astype(jnp.float32)
        outputs.append(summed.astype(jnp.bfloat16))
    attended = jnp.stack(outputs, axis=0).reshape(-1, outputs[0].shape[1])

    cache_width = 2 * HD // sharing
    cache_column = tp_rank % sharing * cache_width
    slots_here = row_count // PAGE
    page_total = page_slots.shape[0]
    wanted = seq_rank * slots_here + jnp.arange(slots_here, dtype=jnp.int32)
    page_of_slot = jnp.sum(
        jnp.where(
            page_slots[None, :] == wanted[:, None],
            jnp.arange(page_total, dtype=jnp.int32)[None, :],
            0,
        ),
        axis=1,
    )
    pages = [
        lax.dynamic_slice(gathered, (page_of_slot[j] * PAGE, cache_column), (PAGE, cache_width))
        for j in range(slots_here)
    ]
    cache_here = jnp.stack(pages, axis=0)
    return (attended, cache_here)


def solution(mesh):
    seq_size, tp_size = mesh.devices.shape
    split_mesh = jax.sharding.Mesh(
        mesh.devices.reshape(seq_size, tp_size // 2, 2), ("seq", "tpz", "tpx")
    )
    tp = ("tpz", "tpx")
    placed = (P("seq", None), P(), P(None, tp), P(), P(), P(tp, None), P(), P())
    return jax.shard_map(
        on_device,
        mesh=split_mesh,
        in_specs=placed,
        out_specs=(P(("seq",) + tp, None), P("seq", None, tp)),
        check_vma=False,
    )
```

```python
import functools

import jax
import jax.numpy as jnp
from jax import lax
from jax.experimental import pallas as pl
from jax.experimental.pallas import tpu as pltpu
from jax.sharding import PartitionSpec as P

HD = 128
PAGE = 128
BQ = 256
CHUNKS = 2
BK = 1024


epsilon = 1e-05
rope_base = 5000000.0


def segment_start(token_index, prompt_lengths):
    prompt_ends = jnp.cumsum(prompt_lengths)
    finished = prompt_ends[None, :] <= token_index[:, None]
    return jnp.sum(jnp.where(finished, prompt_lengths[None, :], 0), axis=1)


def rotate(vectors, position):
    half_size = HD // 2
    frequency = rope_base ** (-(2.0 * jnp.arange(half_size, dtype=jnp.float32)) / HD)
    angle = position.astype(jnp.float32)[:, None] * frequency[None, :]
    cosine = jnp.cos(angle)[:, None, :]
    sine = jnp.sin(angle)[:, None, :]
    first_half = vectors[..., :half_size]
    second_half = vectors[..., half_size:]
    return jnp.concatenate(
        [first_half * cosine - second_half * sine, second_half * cosine + first_half * sine],
        axis=-1,
    )


def normalize(tokens, norm_gain):
    hidden = tokens.astype(jnp.float32)
    factor = lax.rsqrt(jnp.mean(hidden * hidden, axis=-1, keepdims=True) + epsilon)
    return (hidden * factor * norm_gain.astype(jnp.float32)).astype(jnp.bfloat16)


def flash_kernel(lo_ref, hi_ref, base_ref, last_start_ref, q_ref, start_ref, index_ref, kv_ref, o_ref):
    i = pl.program_id(0)
    heads = q_ref.shape[1] // HD
    row_index = index_ref[...]
    row_start = start_ref[...]
    scale = HD ** (-0.5)

    def step(kb, carry, masked):
        offset = pl.multiple_of(kb * BK, BK)
        keys = kv_ref[pl.ds(offset, BK), pl.ds(0, HD)]
        values = kv_ref[pl.ds(offset, BK), pl.ds(HD, HD)]
        if masked:
            key_index = offset + lax.broadcasted_iota(jnp.int32, (1, BK), 1)
            visible = (key_index >= row_start) & (key_index <= row_index)
        updated = []
        for h in range(heads):
            running_max, running_sum, weighted = carry[h]
            q = q_ref[:, pl.ds(h * HD, HD)]
            scores = lax.dot_general(
                q, keys, (((1,), (1,)), ((), ())), preferred_element_type=jnp.float32
            ) * scale
            if masked:
                scores = jnp.where(visible, scores, -1e30)
            fresh_max = jnp.maximum(running_max, jnp.max(scores, axis=1, keepdims=True))
            weights = jnp.exp(scores - fresh_max)
            if masked:
                weights = jnp.where(visible, weights, 0.0)
            shrink = jnp.exp(running_max - fresh_max)
            running_sum = running_sum * shrink + jnp.sum(weights, axis=1, keepdims=True)
            weighted = weighted * shrink + jnp.dot(
                weights.astype(jnp.bfloat16), values, preferred_element_type=jnp.float32
            )
            updated.append((fresh_max, running_sum, weighted))
        return tuple(updated)

    lo = lo_ref[i]
    hi = hi_ref[i] + 1
    full_lo = (last_start_ref[i] + BK - 1) // BK
    full_hi = (base_ref[i] + 1) // BK
    mid_lo = jnp.minimum(jnp.maximum(full_lo, lo), hi)
    mid_hi = jnp.maximum(mid_lo, jnp.minimum(full_hi, hi))
    carry = tuple(
        (
            jnp.full((BQ, 1), -1e30, jnp.float32),
            jnp.zeros((BQ, 1), jnp.float32),
            jnp.zeros((BQ, HD), jnp.float32),
        )
        for h in range(heads)
    )
    before = mid_lo - lo

    def masked_step(j, carry):
        kb = jnp.where(j < before, lo + j, mid_hi + j - before)
        return step(kb, carry, masked=True)

    carry = lax.fori_loop(0, before + hi - mid_hi, masked_step, carry)
    carry = lax.fori_loop(mid_lo, mid_hi, functools.partial(step, masked=False), carry)
    for h in range(heads):
        running_max, running_sum, weighted = carry[h]
        o_ref[:, pl.ds(h * HD, HD)] = (weighted / running_sum).astype(o_ref.dtype)


def flash_attention(queries, row_start, row_index, key_values, bounds):
    rows, width = queries.shape
    q_blocks = rows // BQ
    kv_rows = key_values.shape[0]
    rows_of = lambda i, *_: (i, 0)
    grid_spec = pltpu.PrefetchScalarGridSpec(
        num_scalar_prefetch=4,
        grid=(q_blocks,),
        in_specs=[
            pl.BlockSpec((BQ, width), rows_of),
            pl.BlockSpec((BQ, 1), rows_of),
            pl.BlockSpec((BQ, 1), rows_of),
            pl.BlockSpec((kv_rows, 2 * HD), lambda i, *_: (0, 0)),
        ],
        out_specs=pl.BlockSpec((BQ, width), rows_of),
    )
    return pl.pallas_call(
        flash_kernel,
        grid_spec=grid_spec,
        out_shape=jax.ShapeDtypeStruct((rows, width), jnp.bfloat16),
    )(*bounds, queries, row_start, row_index, key_values)


def on_device(tokens, norm_gain, w_query, w_key, w_value, w_out, prompt_lengths, page_slots):
    row_count = tokens.shape[0]
    tp_count = lax.axis_size("tpz") * lax.axis_size("tpx")
    seq_rank = lax.axis_index("seq")
    tp_rank = lax.axis_index("tpz") * lax.axis_size("tpx") + lax.axis_index("tpx")
    heads_here = w_query.shape[1] // HD
    kv_heads = w_key.shape[1] // HD
    sharing = tp_count // kv_heads
    kv_head = tp_rank // sharing
    token_index = seq_rank * row_count + jnp.arange(row_count, dtype=jnp.int32)
    start = segment_start(token_index, prompt_lengths)
    position = token_index - start
    normed = normalize(tokens, norm_gain)

    key_columns = lax.dynamic_slice_in_dim(w_key, kv_head * HD, HD, 1)
    value_columns = lax.dynamic_slice_in_dim(w_value, kv_head * HD, HD, 1)
    keys_here = rotate(
        jnp.dot(normed, key_columns, preferred_element_type=jnp.float32)[:, None, :], position
    )[:, 0].astype(jnp.bfloat16)
    values_here = jnp.dot(normed, value_columns, preferred_element_type=jnp.float32).astype(
        jnp.bfloat16
    )
    keys_values = jnp.concatenate([keys_here, values_here], axis=1)
    gathered = lax.all_gather(keys_values, "seq", axis=0, tiled=True)

    queries = rotate(
        jnp.dot(normed, w_query, preferred_element_type=jnp.float32).reshape(
            row_count, heads_here, HD
        ),
        position,
    ).astype(jnp.bfloat16).reshape(row_count, heads_here * HD)

    piece = row_count // tp_count // CHUNKS
    chunk_queries = queries.reshape(tp_count, CHUNKS, piece, heads_here * HD)
    chunk_start = start.reshape(tp_count, CHUNKS, piece)
    chunk_index = token_index.reshape(tp_count, CHUNKS, piece)
    chunk_inputs = []
    for c in range(CHUNKS):
        q_rows = chunk_queries[:, c].reshape(tp_count * piece, heads_here * HD)
        s_rows = chunk_start[:, c].reshape(tp_count * piece)
        i_rows = chunk_index[:, c].reshape(tp_count * piece)
        bounds = (s_rows[:1] // BK, i_rows[-1:] // BK, i_rows[:1], s_rows[-1:])
        chunk_inputs.append((q_rows, s_rows[:, None], i_rows[:, None], bounds))
    chunk_inputs = lax.optimization_barrier(chunk_inputs)
    outputs = []
    for q_rows, s_rows, i_rows, bounds in chunk_inputs:
        heads_out = flash_attention(q_rows, s_rows, i_rows, gathered, bounds)
        partial_out = jnp.dot(heads_out, w_out, preferred_element_type=jnp.float32).astype(
            jnp.bfloat16
        )
        received = lax.all_to_all(
            partial_out, ("tpz", "tpx"), split_axis=0, concat_axis=0, tiled=True
        ).reshape(tp_count, piece, -1)
        summed = received[0].astype(jnp.float32)
        for t in range(1, tp_count):
            summed = summed + received[t].astype(jnp.float32)
        outputs.append(summed.astype(jnp.bfloat16))
    attended = jnp.stack(outputs, axis=0).reshape(-1, outputs[0].shape[1])

    cache_width = 2 * HD // sharing
    cache_column = tp_rank % sharing * cache_width
    slots_here = row_count // PAGE
    page_total = page_slots.shape[0]
    wanted = seq_rank * slots_here + jnp.arange(slots_here, dtype=jnp.int32)
    page_of_slot = jnp.sum(
        jnp.where(
            page_slots[None, :] == wanted[:, None],
            jnp.arange(page_total, dtype=jnp.int32)[None, :],
            0,
        ),
        axis=1,
    )
    pages = [
        lax.dynamic_slice(gathered, (page_of_slot[j] * PAGE, cache_column), (PAGE, cache_width))
        for j in range(slots_here)
    ]
    cache_here = jnp.stack(pages, axis=0)
    return (attended, cache_here)


def solution(mesh):
    seq_size, tp_size = mesh.devices.shape
    split_mesh = jax.sharding.Mesh(
        mesh.devices.reshape(seq_size, tp_size // 2, 2), ("seq", "tpz", "tpx")
    )
    tp = ("tpz", "tpx")
    placed = (P("seq", None), P(), P(None, tp), P(), P(), P(tp, None), P(), P())
    return jax.shard_map(
        on_device,
        mesh=split_mesh,
        in_specs=placed,
        out_specs=(P(("seq",) + tp, None), P("seq", None, tp)),
        check_vma=False,
    )
```

```python
import functools

import jax
import jax.numpy as jnp
from jax import lax
from jax.experimental import pallas as pl
from jax.experimental.pallas import tpu as pltpu
from jax.sharding import PartitionSpec as P

HD = 128
PAGE = 128
BQ = 256
CHUNKS = 2
BK = 1024


epsilon = 1e-05
rope_base = 5000000.0


def segment_start(token_index, prompt_lengths):
    prompt_ends = jnp.cumsum(prompt_lengths)
    finished = prompt_ends[None, :] <= token_index[:, None]
    return jnp.sum(jnp.where(finished, prompt_lengths[None, :], 0), axis=1)


def rotate(vectors, position):
    half_size = HD // 2
    frequency = rope_base ** (-(2.0 * jnp.arange(half_size, dtype=jnp.float32)) / HD)
    angle = position.astype(jnp.float32)[:, None] * frequency[None, :]
    cosine = jnp.cos(angle)[:, None, :]
    sine = jnp.sin(angle)[:, None, :]
    first_half = vectors[..., :half_size]
    second_half = vectors[..., half_size:]
    return jnp.concatenate(
        [first_half * cosine - second_half * sine, second_half * cosine + first_half * sine],
        axis=-1,
    )


def normalize(tokens, norm_gain):
    hidden = tokens.astype(jnp.float32)
    factor = lax.rsqrt(jnp.mean(hidden * hidden, axis=-1, keepdims=True) + epsilon)
    return (hidden * factor * norm_gain.astype(jnp.float32)).astype(jnp.bfloat16)


def flash_kernel(lo_ref, hi_ref, base_ref, last_start_ref, q_ref, start_ref, index_ref, kv_ref, o_ref):
    i = pl.program_id(0)
    heads = q_ref.shape[1] // HD
    row_index = index_ref[...]
    row_start = start_ref[...]
    scale = HD ** (-0.5)

    def step(kb, carry, masked):
        offset = pl.multiple_of(kb * BK, BK)
        keys = kv_ref[pl.ds(offset, BK), pl.ds(0, HD)]
        values = kv_ref[pl.ds(offset, BK), pl.ds(HD, HD)]
        if masked:
            key_index = offset + lax.broadcasted_iota(jnp.int32, (1, BK), 1)
            visible = (key_index >= row_start) & (key_index <= row_index)
        updated = []
        for h in range(heads):
            running_max, running_sum, weighted = carry[h]
            q = q_ref[:, pl.ds(h * HD, HD)]
            scores = lax.dot_general(
                q, keys, (((1,), (1,)), ((), ())), preferred_element_type=jnp.float32
            ) * scale
            if masked:
                scores = jnp.where(visible, scores, -1e30)
            fresh_max = jnp.maximum(running_max, jnp.max(scores, axis=1, keepdims=True))
            weights = jnp.exp(scores - fresh_max)
            if masked:
                weights = jnp.where(visible, weights, 0.0)
            shrink = jnp.exp(running_max - fresh_max)
            running_sum = running_sum * shrink + jnp.sum(weights, axis=1, keepdims=True)
            weighted = weighted * shrink + jnp.dot(
                weights.astype(jnp.bfloat16), values, preferred_element_type=jnp.float32
            )
            updated.append((fresh_max, running_sum, weighted))
        return tuple(updated)

    lo = lo_ref[i]
    hi = hi_ref[i] + 1
    full_lo = (last_start_ref[i] + BK - 1) // BK
    full_hi = (base_ref[i] + 1) // BK
    mid_lo = jnp.minimum(jnp.maximum(full_lo, lo), hi)
    mid_hi = jnp.maximum(mid_lo, jnp.minimum(full_hi, hi))
    carry = tuple(
        (
            jnp.full((BQ, 1), -1e30, jnp.float32),
            jnp.zeros((BQ, 1), jnp.float32),
            jnp.zeros((BQ, HD), jnp.float32),
        )
        for h in range(heads)
    )
    before = mid_lo - lo

    def masked_step(j, carry):
        kb = jnp.where(j < before, lo + j, mid_hi + j - before)
        return step(kb, carry, masked=True)

    carry = lax.fori_loop(0, before + hi - mid_hi, masked_step, carry)
    carry = lax.fori_loop(mid_lo, mid_hi, functools.partial(step, masked=False), carry)
    for h in range(heads):
        running_max, running_sum, weighted = carry[h]
        o_ref[:, pl.ds(h * HD, HD)] = (weighted / running_sum).astype(o_ref.dtype)


def flash_attention(queries, row_start, row_index, key_values, bounds):
    rows, width = queries.shape
    q_blocks = rows // BQ
    kv_rows = key_values.shape[0]
    rows_of = lambda i, *_: (i, 0)
    grid_spec = pltpu.PrefetchScalarGridSpec(
        num_scalar_prefetch=4,
        grid=(q_blocks,),
        in_specs=[
            pl.BlockSpec((BQ, width), rows_of),
            pl.BlockSpec((BQ, 1), rows_of),
            pl.BlockSpec((BQ, 1), rows_of),
            pl.BlockSpec((kv_rows, 2 * HD), lambda i, *_: (0, 0)),
        ],
        out_specs=pl.BlockSpec((BQ, width), rows_of),
    )
    return pl.pallas_call(
        flash_kernel,
        grid_spec=grid_spec,
        out_shape=jax.ShapeDtypeStruct((rows, width), jnp.bfloat16),
    )(*bounds, queries, row_start, row_index, key_values)


def on_device(tokens, norm_gain, w_query, w_key, w_value, w_out, prompt_lengths, page_slots):
    row_count = tokens.shape[0]
    tp_count = lax.axis_size("tpz") * lax.axis_size("tpx")
    seq_rank = lax.axis_index("seqc") * lax.axis_size("core") + lax.axis_index("core")
    tp_rank = lax.axis_index("tpz") * lax.axis_size("tpx") + lax.axis_index("tpx")
    heads_here = w_query.shape[1] // HD
    kv_heads = w_key.shape[1] // HD
    sharing = tp_count // kv_heads
    kv_head = tp_rank // sharing
    token_index = seq_rank * row_count + jnp.arange(row_count, dtype=jnp.int32)
    start = segment_start(token_index, prompt_lengths)
    position = token_index - start
    normed = normalize(tokens, norm_gain)

    key_columns = lax.dynamic_slice_in_dim(w_key, kv_head * HD, HD, 1)
    value_columns = lax.dynamic_slice_in_dim(w_value, kv_head * HD, HD, 1)
    keys_here = rotate(
        jnp.dot(normed, key_columns, preferred_element_type=jnp.float32)[:, None, :], position
    )[:, 0].astype(jnp.bfloat16)
    values_here = jnp.dot(normed, value_columns, preferred_element_type=jnp.float32).astype(
        jnp.bfloat16
    )
    keys_values = jnp.concatenate([keys_here, values_here], axis=1)
    gathered = lax.all_gather(keys_values, "seqc", axis=0, tiled=False)
    gathered = lax.all_gather(gathered, "core", axis=1, tiled=False)
    gathered = gathered.reshape(-1, keys_values.shape[1])

    queries = rotate(
        jnp.dot(normed, w_query, preferred_element_type=jnp.float32).reshape(
            row_count, heads_here, HD
        ),
        position,
    ).astype(jnp.bfloat16).reshape(row_count, heads_here * HD)

    piece = row_count // tp_count // CHUNKS
    chunk_queries = queries.reshape(tp_count, CHUNKS, piece, heads_here * HD)
    chunk_start = start.reshape(tp_count, CHUNKS, piece)
    chunk_index = token_index.reshape(tp_count, CHUNKS, piece)
    chunk_inputs = []
    for c in range(CHUNKS):
        q_rows = chunk_queries[:, c].reshape(tp_count * piece, heads_here * HD)
        s_rows = chunk_start[:, c].reshape(tp_count * piece)
        i_rows = chunk_index[:, c].reshape(tp_count * piece)
        bounds = (s_rows[:1] // BK, i_rows[-1:] // BK, i_rows[:1], s_rows[-1:])
        chunk_inputs.append((q_rows, s_rows[:, None], i_rows[:, None], bounds))
    chunk_inputs = lax.optimization_barrier(chunk_inputs)
    outputs = []
    for q_rows, s_rows, i_rows, bounds in chunk_inputs:
        heads_out = flash_attention(q_rows, s_rows, i_rows, gathered, bounds)
        partial_out = jnp.dot(heads_out, w_out, preferred_element_type=jnp.float32).astype(
            jnp.bfloat16
        )
        received = lax.all_to_all(
            partial_out, ("tpz", "tpx"), split_axis=0, concat_axis=0, tiled=True
        ).reshape(tp_count, piece, -1)
        summed = received[0].astype(jnp.float32)
        for t in range(1, tp_count):
            summed = summed + received[t].astype(jnp.float32)
        outputs.append(summed.astype(jnp.bfloat16))
    attended = jnp.stack(outputs, axis=0).reshape(-1, outputs[0].shape[1])

    cache_width = 2 * HD // sharing
    cache_column = tp_rank % sharing * cache_width
    slots_here = row_count // PAGE
    page_total = page_slots.shape[0]
    wanted = seq_rank * slots_here + jnp.arange(slots_here, dtype=jnp.int32)
    page_of_slot = jnp.sum(
        jnp.where(
            page_slots[None, :] == wanted[:, None],
            jnp.arange(page_total, dtype=jnp.int32)[None, :],
            0,
        ),
        axis=1,
    )
    pages = [
        lax.dynamic_slice(gathered, (page_of_slot[j] * PAGE, cache_column), (PAGE, cache_width))
        for j in range(slots_here)
    ]
    cache_here = jnp.stack(pages, axis=0)
    return (attended, cache_here)


def solution(mesh):
    seq_size, tp_size = mesh.devices.shape
    split_mesh = jax.sharding.Mesh(
        mesh.devices.reshape(seq_size // 2, 2, tp_size // 2, 2), ("seqc", "core", "tpz", "tpx")
    )
    seq = ("seqc", "core")
    tp = ("tpz", "tpx")
    placed = (P(seq, None), P(), P(None, tp), P(), P(), P(tp, None), P(), P())
    return jax.shard_map(
        on_device,
        mesh=split_mesh,
        in_specs=placed,
        out_specs=(P(seq + tp, None), P(seq, None, tp)),
        check_vma=False,
    )
```

```python
import functools

import jax
import jax.numpy as jnp
from jax import lax
from jax.experimental import pallas as pl
from jax.experimental.pallas import tpu as pltpu
from jax.sharding import PartitionSpec as P

HD = 128
PAGE = 128
BQ = 256
CHUNKS = 2
BK = 1024


epsilon = 1e-05
rope_base = 5000000.0


def segment_start(token_index, prompt_lengths):
    prompt_ends = jnp.cumsum(prompt_lengths)
    finished = prompt_ends[None, :] <= token_index[:, None]
    return jnp.sum(jnp.where(finished, prompt_lengths[None, :], 0), axis=1)


def rotate(vectors, position):
    half_size = HD // 2
    frequency = rope_base ** (-(2.0 * jnp.arange(half_size, dtype=jnp.float32)) / HD)
    angle = position.astype(jnp.float32)[:, None] * frequency[None, :]
    cosine = jnp.cos(angle)[:, None, :]
    sine = jnp.sin(angle)[:, None, :]
    first_half = vectors[..., :half_size]
    second_half = vectors[..., half_size:]
    return jnp.concatenate(
        [first_half * cosine - second_half * sine, second_half * cosine + first_half * sine],
        axis=-1,
    )


def normalize(tokens, norm_gain):
    hidden = tokens.astype(jnp.float32)
    factor = lax.rsqrt(jnp.mean(hidden * hidden, axis=-1, keepdims=True) + epsilon)
    return (hidden * factor * norm_gain.astype(jnp.float32)).astype(jnp.bfloat16)


def flash_kernel(lo_ref, hi_ref, base_ref, last_start_ref, q_ref, start_ref, index_ref, kv_ref, o_ref):
    i = pl.program_id(0)
    heads = q_ref.shape[1] // HD
    row_index = index_ref[...]
    row_start = start_ref[...]
    scale = HD ** (-0.5)

    def step(kb, carry, masked):
        offset = pl.multiple_of(kb * BK, BK)
        keys = kv_ref[pl.ds(offset, BK), pl.ds(0, HD)]
        values = kv_ref[pl.ds(offset, BK), pl.ds(HD, HD)]
        values_ones = jnp.concatenate([values, jnp.ones((BK, HD), values.dtype)], axis=1)
        if masked:
            key_index = offset + lax.broadcasted_iota(jnp.int32, (1, BK), 1)
            visible = (key_index >= row_start) & (key_index <= row_index)
        updated = []
        for h in range(heads):
            running_max, running_sum, weighted = carry[h]
            q = q_ref[:, pl.ds(h * HD, HD)]
            scores = lax.dot_general(
                q, keys, (((1,), (1,)), ((), ())), preferred_element_type=jnp.float32
            ) * scale
            if masked:
                scores = jnp.where(visible, scores, -1e30)
            fresh_max = jnp.maximum(running_max, jnp.max(scores, axis=1, keepdims=True))
            weights = jnp.exp(scores - fresh_max)
            if masked:
                weights = jnp.where(visible, weights, 0.0)
            shrink = jnp.exp(running_max - fresh_max)
            both = jnp.dot(
                weights.astype(jnp.bfloat16), values_ones, preferred_element_type=jnp.float32
            )
            running_sum = running_sum * shrink + both[:, HD:]
            weighted = weighted * shrink + both[:, :HD]
            updated.append((fresh_max, running_sum, weighted))
        return tuple(updated)

    lo = lo_ref[i]
    hi = hi_ref[i] + 1
    full_lo = (last_start_ref[i] + BK - 1) // BK
    full_hi = (base_ref[i] + 1) // BK
    mid_lo = jnp.minimum(jnp.maximum(full_lo, lo), hi)
    mid_hi = jnp.maximum(mid_lo, jnp.minimum(full_hi, hi))
    carry = tuple(
        (
            jnp.full((BQ, 1), -1e30, jnp.float32),
            jnp.zeros((BQ, HD), jnp.float32),
            jnp.zeros((BQ, HD), jnp.float32),
        )
        for h in range(heads)
    )
    before = mid_lo - lo

    def masked_step(j, carry):
        kb = jnp.where(j < before, lo + j, mid_hi + j - before)
        return step(kb, carry, masked=True)

    carry = lax.fori_loop(0, before + hi - mid_hi, masked_step, carry)
    carry = lax.fori_loop(mid_lo, mid_hi, functools.partial(step, masked=False), carry)
    for h in range(heads):
        running_max, running_sum, weighted = carry[h]
        o_ref[:, pl.ds(h * HD, HD)] = (weighted / running_sum).astype(o_ref.dtype)


def flash_attention(queries, row_start, row_index, key_values, bounds):
    rows, width = queries.shape
    q_blocks = rows // BQ
    kv_rows = key_values.shape[0]
    rows_of = lambda i, *_: (i, 0)
    grid_spec = pltpu.PrefetchScalarGridSpec(
        num_scalar_prefetch=4,
        grid=(q_blocks,),
        in_specs=[
            pl.BlockSpec((BQ, width), rows_of),
            pl.BlockSpec((BQ, 1), rows_of),
            pl.BlockSpec((BQ, 1), rows_of),
            pl.BlockSpec((kv_rows, 2 * HD), lambda i, *_: (0, 0)),
        ],
        out_specs=pl.BlockSpec((BQ, width), rows_of),
    )
    return pl.pallas_call(
        flash_kernel,
        grid_spec=grid_spec,
        out_shape=jax.ShapeDtypeStruct((rows, width), jnp.bfloat16),
    )(*bounds, queries, row_start, row_index, key_values)


def on_device(tokens, norm_gain, w_query, w_key, w_value, w_out, prompt_lengths, page_slots):
    row_count = tokens.shape[0]
    tp_count = lax.axis_size("tpz") * lax.axis_size("tpx")
    seq_rank = lax.axis_index("seq")
    tp_rank = lax.axis_index("tpz") * lax.axis_size("tpx") + lax.axis_index("tpx")
    heads_here = w_query.shape[1] // HD
    kv_heads = w_key.shape[1] // HD
    sharing = tp_count // kv_heads
    kv_head = tp_rank // sharing
    token_index = seq_rank * row_count + jnp.arange(row_count, dtype=jnp.int32)
    start = segment_start(token_index, prompt_lengths)
    position = token_index - start
    normed = normalize(tokens, norm_gain)

    key_columns = lax.dynamic_slice_in_dim(w_key, kv_head * HD, HD, 1)
    value_columns = lax.dynamic_slice_in_dim(w_value, kv_head * HD, HD, 1)
    keys_here = rotate(
        jnp.dot(normed, key_columns, preferred_element_type=jnp.float32)[:, None, :], position
    )[:, 0].astype(jnp.bfloat16)
    values_here = jnp.dot(normed, value_columns, preferred_element_type=jnp.float32).astype(
        jnp.bfloat16
    )
    keys_values = jnp.concatenate([keys_here, values_here], axis=1)
    gathered = lax.all_gather(keys_values, "seq", axis=0, tiled=True)

    queries = rotate(
        jnp.dot(normed, w_query, preferred_element_type=jnp.float32).reshape(
            row_count, heads_here, HD
        ),
        position,
    ).astype(jnp.bfloat16).reshape(row_count, heads_here * HD)

    piece = row_count // tp_count // CHUNKS
    chunk_queries = queries.reshape(tp_count, CHUNKS, piece, heads_here * HD)
    chunk_start = start.reshape(tp_count, CHUNKS, piece)
    chunk_index = token_index.reshape(tp_count, CHUNKS, piece)
    chunk_inputs = []
    for c in range(CHUNKS):
        q_rows = chunk_queries[:, c].reshape(tp_count * piece, heads_here * HD)
        s_rows = chunk_start[:, c].reshape(tp_count * piece)
        i_rows = chunk_index[:, c].reshape(tp_count * piece)
        bounds = (s_rows[:1] // BK, i_rows[-1:] // BK, i_rows[:1], s_rows[-1:])
        chunk_inputs.append((q_rows, s_rows[:, None], i_rows[:, None], bounds))
    chunk_inputs = lax.optimization_barrier(chunk_inputs)
    outputs = []
    for q_rows, s_rows, i_rows, bounds in chunk_inputs:
        heads_out = flash_attention(q_rows, s_rows, i_rows, gathered, bounds)
        partial_out = jnp.dot(heads_out, w_out, preferred_element_type=jnp.float32).astype(
            jnp.bfloat16
        )
        received = lax.all_to_all(
            partial_out, ("tpz", "tpx"), split_axis=0, concat_axis=0, tiled=True
        ).reshape(tp_count, piece, -1)
        summed = received[0].astype(jnp.float32)
        for t in range(1, tp_count):
            summed = summed + received[t].astype(jnp.float32)
        outputs.append(summed.astype(jnp.bfloat16))
    attended = jnp.stack(outputs, axis=0).reshape(-1, outputs[0].shape[1])

    cache_width = 2 * HD // sharing
    cache_column = tp_rank % sharing * cache_width
    slots_here = row_count // PAGE
    page_total = page_slots.shape[0]
    wanted = seq_rank * slots_here + jnp.arange(slots_here, dtype=jnp.int32)
    page_of_slot = jnp.sum(
        jnp.where(
            page_slots[None, :] == wanted[:, None],
            jnp.arange(page_total, dtype=jnp.int32)[None, :],
            0,
        ),
        axis=1,
    )
    pages = [
        lax.dynamic_slice(gathered, (page_of_slot[j] * PAGE, cache_column), (PAGE, cache_width))
        for j in range(slots_here)
    ]
    cache_here = jnp.stack(pages, axis=0)
    return (attended, cache_here)


def solution(mesh):
    seq_size, tp_size = mesh.devices.shape
    split_mesh = jax.sharding.Mesh(
        mesh.devices.reshape(seq_size, tp_size // 2, 2), ("seq", "tpz", "tpx")
    )
    tp = ("tpz", "tpx")
    placed = (P("seq", None), P(), P(None, tp), P(), P(), P(tp, None), P(), P())
    return jax.shard_map(
        on_device,
        mesh=split_mesh,
        in_specs=placed,
        out_specs=(P(("seq",) + tp, None), P("seq", None, tp)),
        check_vma=False,
    )
```

```python
import functools

import jax
import jax.numpy as jnp
from jax import lax
from jax.experimental import pallas as pl
from jax.experimental.pallas import tpu as pltpu
from jax.sharding import PartitionSpec as P

HD = 128
PAGE = 128
BQ = 256
CHUNKS = 2
BK = 1024


epsilon = 1e-05
rope_base = 5000000.0


def segment_start(token_index, prompt_lengths):
    prompt_ends = jnp.cumsum(prompt_lengths)
    finished = prompt_ends[None, :] <= token_index[:, None]
    return jnp.sum(jnp.where(finished, prompt_lengths[None, :], 0), axis=1)


def rotate(vectors, position):
    half_size = HD // 2
    frequency = rope_base ** (-(2.0 * jnp.arange(half_size, dtype=jnp.float32)) / HD)
    angle = position.astype(jnp.float32)[:, None] * frequency[None, :]
    cosine = jnp.cos(angle)[:, None, :]
    sine = jnp.sin(angle)[:, None, :]
    first_half = vectors[..., :half_size]
    second_half = vectors[..., half_size:]
    return jnp.concatenate(
        [first_half * cosine - second_half * sine, second_half * cosine + first_half * sine],
        axis=-1,
    )


def normalize(tokens, norm_gain):
    hidden = tokens.astype(jnp.float32)
    factor = lax.rsqrt(jnp.mean(hidden * hidden, axis=-1, keepdims=True) + epsilon)
    return (hidden * factor * norm_gain.astype(jnp.float32)).astype(jnp.bfloat16)


def flash_kernel(lo_ref, hi_ref, base_ref, last_start_ref, q_ref, start_ref, index_ref, kv_ref, o_ref):
    i = pl.program_id(0)
    heads = q_ref.shape[1] // HD
    row_index = index_ref[...]
    row_start = start_ref[...]
    scale = HD ** (-0.5)

    def step(kb, carry, masked):
        offset = pl.multiple_of(kb * BK, BK)
        keys = kv_ref[pl.ds(offset, BK), pl.ds(0, HD)]
        values = kv_ref[pl.ds(offset, BK), pl.ds(HD, HD)]
        values_ones = jnp.concatenate([values, jnp.ones((BK, HD), values.dtype)], axis=1)
        if masked:
            key_index = offset + lax.broadcasted_iota(jnp.int32, (1, BK), 1)
            visible = (key_index >= row_start) & (key_index <= row_index)
        updated = []
        for h in range(heads):
            running_max, running_sum, weighted = carry[h]
            q = q_ref[:, pl.ds(h * HD, HD)]
            scores = lax.dot_general(
                q, keys, (((1,), (1,)), ((), ())), preferred_element_type=jnp.float32
            ) * scale
            if masked:
                scores = jnp.where(visible, scores, -1e30)
            fresh_max = jnp.maximum(running_max, jnp.max(scores, axis=1, keepdims=True))
            weights = jnp.exp(scores - fresh_max)
            if masked:
                weights = jnp.where(visible, weights, 0.0)
            shrink = jnp.exp(running_max - fresh_max)
            both = jnp.dot(
                weights.astype(jnp.bfloat16), values_ones, preferred_element_type=jnp.float32
            )
            running_sum = running_sum * shrink + both[:, HD:]
            weighted = weighted * shrink + both[:, :HD]
            updated.append((fresh_max, running_sum, weighted))
        return tuple(updated)

    lo = lo_ref[i]
    hi = hi_ref[i] + 1
    full_lo = (last_start_ref[i] + BK - 1) // BK
    full_hi = (base_ref[i] + 1) // BK
    mid_lo = jnp.minimum(jnp.maximum(full_lo, lo), hi)
    mid_hi = jnp.maximum(mid_lo, jnp.minimum(full_hi, hi))
    carry = tuple(
        (
            jnp.full((BQ, 1), -1e30, jnp.float32),
            jnp.zeros((BQ, HD), jnp.float32),
            jnp.zeros((BQ, HD), jnp.float32),
        )
        for h in range(heads)
    )
    before = mid_lo - lo

    def masked_step(j, carry):
        kb = jnp.where(j < before, lo + j, mid_hi + j - before)
        return step(kb, carry, masked=True)

    carry = lax.fori_loop(0, before + hi - mid_hi, masked_step, carry)
    carry = lax.fori_loop(mid_lo, mid_hi, functools.partial(step, masked=False), carry)
    for h in range(heads):
        running_max, running_sum, weighted = carry[h]
        o_ref[:, pl.ds(h * HD, HD)] = (weighted / running_sum).astype(o_ref.dtype)


def flash_attention(queries, row_start, row_index, key_values, bounds):
    rows, width = queries.shape
    q_blocks = rows // BQ
    kv_rows = key_values.shape[0]
    rows_of = lambda i, *_: (i, 0)
    grid_spec = pltpu.PrefetchScalarGridSpec(
        num_scalar_prefetch=4,
        grid=(q_blocks,),
        in_specs=[
            pl.BlockSpec((BQ, width), rows_of),
            pl.BlockSpec((BQ, 1), rows_of),
            pl.BlockSpec((BQ, 1), rows_of),
            pl.BlockSpec((kv_rows, 2 * HD), lambda i, *_: (0, 0)),
        ],
        out_specs=pl.BlockSpec((BQ, width), rows_of),
    )
    return pl.pallas_call(
        flash_kernel,
        grid_spec=grid_spec,
        out_shape=jax.ShapeDtypeStruct((rows, width), jnp.bfloat16),
    )(*bounds, queries, row_start, row_index, key_values)


def on_device(tokens, norm_gain, w_query, w_key, w_value, w_out, prompt_lengths, page_slots):
    row_count = tokens.shape[0]
    tp_count = lax.axis_size("tpz") * lax.axis_size("tpx")
    seq_rank = lax.axis_index("seq")
    tp_rank = lax.axis_index("tpz") * lax.axis_size("tpx") + lax.axis_index("tpx")
    heads_here = w_query.shape[1] // HD
    kv_heads = w_key.shape[1] // HD
    sharing = tp_count // kv_heads
    kv_head = tp_rank // sharing
    token_index = seq_rank * row_count + jnp.arange(row_count, dtype=jnp.int32)
    start = segment_start(token_index, prompt_lengths)
    position = token_index - start
    normed = normalize(tokens, norm_gain)

    key_columns = lax.dynamic_slice_in_dim(w_key, kv_head * HD, HD, 1)
    value_columns = lax.dynamic_slice_in_dim(w_value, kv_head * HD, HD, 1)
    keys_here = rotate(
        jnp.dot(normed, key_columns, preferred_element_type=jnp.float32)[:, None, :], position
    )[:, 0].astype(jnp.bfloat16)
    values_here = jnp.dot(normed, value_columns, preferred_element_type=jnp.float32).astype(
        jnp.bfloat16
    )
    keys_values = jnp.concatenate([keys_here, values_here], axis=1)
    gathered = lax.all_gather(keys_values, "seq", axis=0, tiled=True)

    queries = rotate(
        jnp.dot(normed, w_query, preferred_element_type=jnp.float32).reshape(
            row_count, heads_here, HD
        ),
        position,
    ).astype(jnp.bfloat16).reshape(row_count, heads_here * HD)

    piece = row_count // tp_count // CHUNKS
    chunk_queries = queries.reshape(tp_count, CHUNKS, piece, heads_here * HD)
    chunk_start = start.reshape(tp_count, CHUNKS, piece)
    chunk_index = token_index.reshape(tp_count, CHUNKS, piece)
    chunk_inputs = []
    for c in range(CHUNKS):
        q_rows = chunk_queries[:, c].reshape(tp_count * piece, heads_here * HD)
        s_rows = chunk_start[:, c].reshape(tp_count * piece)
        i_rows = chunk_index[:, c].reshape(tp_count * piece)
        bounds = (s_rows[:1] // BK, i_rows[-1:] // BK, i_rows[:1], s_rows[-1:])
        chunk_inputs.append((q_rows, s_rows[:, None], i_rows[:, None], bounds))
    chunk_inputs = lax.optimization_barrier(chunk_inputs)
    outputs = []
    for q_rows, s_rows, i_rows, bounds in chunk_inputs:
        heads_out = flash_attention(q_rows, s_rows, i_rows, gathered, bounds)
        partial_out = jnp.dot(heads_out, w_out, preferred_element_type=jnp.float32).astype(
            jnp.bfloat16
        )
        if len(outputs) + 1 < CHUNKS:
            outputs.append(
                lax.psum_scatter(partial_out, ("tpz", "tpx"), scatter_dimension=0, tiled=True)
            )
            continue
        received = lax.all_to_all(
            partial_out, ("tpz", "tpx"), split_axis=0, concat_axis=0, tiled=True
        ).reshape(tp_count, piece, -1)
        summed = received[0].astype(jnp.float32)
        for t in range(1, tp_count):
            summed = summed + received[t].astype(jnp.float32)
        outputs.append(summed.astype(jnp.bfloat16))
    attended = jnp.stack(outputs, axis=0).reshape(-1, outputs[0].shape[1])

    cache_width = 2 * HD // sharing
    cache_column = tp_rank % sharing * cache_width
    slots_here = row_count // PAGE
    page_total = page_slots.shape[0]
    wanted = seq_rank * slots_here + jnp.arange(slots_here, dtype=jnp.int32)
    page_of_slot = jnp.sum(
        jnp.where(
            page_slots[None, :] == wanted[:, None],
            jnp.arange(page_total, dtype=jnp.int32)[None, :],
            0,
        ),
        axis=1,
    )
    pages = [
        lax.dynamic_slice(gathered, (page_of_slot[j] * PAGE, cache_column), (PAGE, cache_width))
        for j in range(slots_here)
    ]
    cache_here = jnp.stack(pages, axis=0)
    return (attended, cache_here)


def solution(mesh):
    seq_size, tp_size = mesh.devices.shape
    split_mesh = jax.sharding.Mesh(
        mesh.devices.reshape(seq_size, tp_size // 2, 2), ("seq", "tpz", "tpx")
    )
    tp = ("tpz", "tpx")
    placed = (P("seq", None), P(), P(None, tp), P(), P(), P(tp, None), P(), P())
    return jax.shard_map(
        on_device,
        mesh=split_mesh,
        in_specs=placed,
        out_specs=(P(("seq",) + tp, None), P("seq", None, tp)),
        check_vma=False,
    )
```

```python
import functools

import jax
import jax.numpy as jnp
from jax import lax
from jax.experimental import pallas as pl
from jax.experimental.pallas import tpu as pltpu
from jax.sharding import PartitionSpec as P

HD = 128
PAGE = 128
BQ = 256
CHUNKS = 2
BK = 1024


epsilon = 1e-05
rope_base = 5000000.0


def segment_start(token_index, prompt_lengths):
    prompt_ends = jnp.cumsum(prompt_lengths)
    finished = prompt_ends[None, :] <= token_index[:, None]
    return jnp.sum(jnp.where(finished, prompt_lengths[None, :], 0), axis=1)


def rotate(vectors, position):
    half_size = HD // 2
    frequency = rope_base ** (-(2.0 * jnp.arange(half_size, dtype=jnp.float32)) / HD)
    angle = position.astype(jnp.float32)[:, None] * frequency[None, :]
    cosine = jnp.cos(angle)[:, None, :]
    sine = jnp.sin(angle)[:, None, :]
    first_half = vectors[..., :half_size]
    second_half = vectors[..., half_size:]
    return jnp.concatenate(
        [first_half * cosine - second_half * sine, second_half * cosine + first_half * sine],
        axis=-1,
    )


def normalize(tokens, norm_gain):
    hidden = tokens.astype(jnp.float32)
    factor = lax.rsqrt(jnp.mean(hidden * hidden, axis=-1, keepdims=True) + epsilon)
    return (hidden * factor * norm_gain.astype(jnp.float32)).astype(jnp.bfloat16)


def flash_kernel(lo_ref, hi_ref, base_ref, last_start_ref, q_ref, start_ref, index_ref, kv_ref, o_ref):
    i = pl.program_id(0)
    heads = q_ref.shape[1] // HD
    row_index = index_ref[...]
    row_start = start_ref[...]
    scale = HD ** (-0.5)

    def step(kb, carry, masked):
        offset = pl.multiple_of(kb * BK, BK)
        keys = kv_ref[pl.ds(offset, BK), pl.ds(0, HD)]
        values = kv_ref[pl.ds(offset, BK), pl.ds(HD, HD)]
        values_ones = jnp.concatenate([values, jnp.ones((BK, HD), values.dtype)], axis=1)
        if masked:
            key_index = offset + lax.broadcasted_iota(jnp.int32, (1, BK), 1)
            visible = (key_index >= row_start) & (key_index <= row_index)
        updated = []
        for h in range(heads):
            running_max, running_sum, weighted = carry[h]
            q = q_ref[:, pl.ds(h * HD, HD)]
            scores = lax.dot_general(
                q, keys, (((1,), (1,)), ((), ())), preferred_element_type=jnp.float32
            ) * scale
            if masked:
                scores = jnp.where(visible, scores, -1e30)
            fresh_max = jnp.maximum(running_max, jnp.max(scores, axis=1, keepdims=True))
            weights = jnp.exp(scores - fresh_max)
            if masked:
                weights = jnp.where(visible, weights, 0.0)
            shrink = jnp.exp(running_max - fresh_max)
            both = jnp.dot(
                weights.astype(jnp.bfloat16), values_ones, preferred_element_type=jnp.float32
            )
            running_sum = running_sum * shrink + both[:, HD:]
            weighted = weighted * shrink + both[:, :HD]
            updated.append((fresh_max, running_sum, weighted))
        return tuple(updated)

    lo = lo_ref[i]
    hi = hi_ref[i] + 1
    full_lo = (last_start_ref[i] + BK - 1) // BK
    full_hi = (base_ref[i] + 1) // BK
    mid_lo = jnp.minimum(jnp.maximum(full_lo, lo), hi)
    mid_hi = jnp.maximum(mid_lo, jnp.minimum(full_hi, hi))
    carry = tuple(
        (
            jnp.full((BQ, 1), -1e30, jnp.float32),
            jnp.zeros((BQ, HD), jnp.float32),
            jnp.zeros((BQ, HD), jnp.float32),
        )
        for h in range(heads)
    )
    before = mid_lo - lo

    def masked_step(j, carry):
        kb = jnp.where(j < before, lo + j, mid_hi + j - before)
        return step(kb, carry, masked=True)

    carry = lax.fori_loop(0, before + hi - mid_hi, masked_step, carry)
    carry = lax.fori_loop(mid_lo, mid_hi, functools.partial(step, masked=False), carry)
    for h in range(heads):
        running_max, running_sum, weighted = carry[h]
        o_ref[:, pl.ds(h * HD, HD)] = (weighted / running_sum).astype(o_ref.dtype)


def flash_attention(queries, row_start, row_index, key_values, bounds):
    rows, width = queries.shape
    q_blocks = rows // BQ
    kv_rows = key_values.shape[0]
    rows_of = lambda i, *_: (i, 0)
    grid_spec = pltpu.PrefetchScalarGridSpec(
        num_scalar_prefetch=4,
        grid=(q_blocks,),
        in_specs=[
            pl.BlockSpec((BQ, width), rows_of),
            pl.BlockSpec((BQ, 1), rows_of),
            pl.BlockSpec((BQ, 1), rows_of),
            pl.BlockSpec((kv_rows, 2 * HD), lambda i, *_: (0, 0)),
        ],
        out_specs=pl.BlockSpec((BQ, width), rows_of),
    )
    return pl.pallas_call(
        flash_kernel,
        grid_spec=grid_spec,
        out_shape=jax.ShapeDtypeStruct((rows, width), jnp.bfloat16),
    )(*bounds, queries, row_start, row_index, key_values)


def on_device(tokens, norm_gain, w_query, w_key, w_value, w_out, prompt_lengths, page_slots):
    row_count = tokens.shape[0]
    tp_count = lax.axis_size("tpz") * lax.axis_size("tpx")
    seq_rank = lax.axis_index("seq")
    tp_rank = lax.axis_index("tpz") * lax.axis_size("tpx") + lax.axis_index("tpx")
    heads_here = w_query.shape[1] // HD
    kv_heads = w_key.shape[1] // HD
    sharing = tp_count // kv_heads
    kv_head = tp_rank // sharing
    token_index = seq_rank * row_count + jnp.arange(row_count, dtype=jnp.int32)
    start = segment_start(token_index, prompt_lengths)
    position = token_index - start
    normed = normalize(tokens, norm_gain)

    key_columns = lax.dynamic_slice_in_dim(w_key, kv_head * HD, HD, 1)
    value_columns = lax.dynamic_slice_in_dim(w_value, kv_head * HD, HD, 1)
    keys_here = rotate(
        jnp.dot(normed, key_columns, preferred_element_type=jnp.float32)[:, None, :], position
    )[:, 0].astype(jnp.bfloat16)
    values_here = jnp.dot(normed, value_columns, preferred_element_type=jnp.float32).astype(
        jnp.bfloat16
    )
    keys_values = jnp.concatenate([keys_here, values_here], axis=1)
    gathered = lax.all_gather(keys_values, "seq", axis=0, tiled=True)

    queries = rotate(
        jnp.dot(normed, w_query, preferred_element_type=jnp.float32).reshape(
            row_count, heads_here, HD
        ),
        position,
    ).astype(jnp.bfloat16).reshape(row_count, heads_here * HD)

    piece = row_count // tp_count // CHUNKS
    chunk_queries = queries.reshape(tp_count, CHUNKS, piece, heads_here * HD)
    chunk_start = start.reshape(tp_count, CHUNKS, piece)
    chunk_index = token_index.reshape(tp_count, CHUNKS, piece)
    seq_count = lax.axis_size("seq")
    swap = [(r, seq_count - 1 - r) for r in range(seq_count)]
    partner_index = (seq_count - 1 - seq_rank) * row_count + jnp.arange(row_count, dtype=jnp.int32)
    partner_start = segment_start(partner_index, prompt_lengths)
    partner_start = partner_start.reshape(tp_count, CHUNKS, piece)
    partner_index = partner_index.reshape(tp_count, CHUNKS, piece)

    def kernel_inputs(q_rows, s_rows, i_rows):
        s_rows = s_rows.reshape(tp_count * piece)
        i_rows = i_rows.reshape(tp_count * piece)
        bounds = (s_rows[:1] // BK, i_rows[-1:] // BK, i_rows[:1], s_rows[-1:])
        return (q_rows.reshape(tp_count * piece, heads_here * HD), s_rows[:, None], i_rows[:, None], bounds)

    sent_queries = lax.ppermute(chunk_queries[:, 1], "seq", swap)
    own_inputs = kernel_inputs(chunk_queries[:, 0], chunk_start[:, 0], chunk_index[:, 0])
    partner_inputs = kernel_inputs(sent_queries, partner_start[:, 1], partner_index[:, 1])
    own_inputs, partner_inputs = lax.optimization_barrier((own_inputs, partner_inputs))
    def reduce_over_tp(heads_out):
        partial_out = jnp.dot(heads_out, w_out, preferred_element_type=jnp.float32).astype(
            jnp.bfloat16
        )
        received = lax.all_to_all(
            partial_out, ("tpz", "tpx"), split_axis=0, concat_axis=0, tiled=True
        ).reshape(tp_count, piece, -1)
        summed = received[0].astype(jnp.float32)
        for t in range(1, tp_count):
            summed = summed + received[t].astype(jnp.float32)
        return summed.astype(jnp.bfloat16)

    partner_heads = flash_attention(*partner_inputs[:3], gathered, partner_inputs[3])
    partner_heads, own_inputs = lax.optimization_barrier((partner_heads, own_inputs))
    returned = lax.ppermute(reduce_over_tp(partner_heads), "seq", swap)
    own_heads = flash_attention(*own_inputs[:3], gathered, own_inputs[3])
    outputs = [reduce_over_tp(own_heads), returned]
    attended = jnp.stack(outputs, axis=0).reshape(-1, outputs[0].shape[1])

    cache_width = 2 * HD // sharing
    cache_column = tp_rank % sharing * cache_width
    slots_here = row_count // PAGE
    page_total = page_slots.shape[0]
    wanted = seq_rank * slots_here + jnp.arange(slots_here, dtype=jnp.int32)
    page_of_slot = jnp.sum(
        jnp.where(
            page_slots[None, :] == wanted[:, None],
            jnp.arange(page_total, dtype=jnp.int32)[None, :],
            0,
        ),
        axis=1,
    )
    pages = [
        lax.dynamic_slice(gathered, (page_of_slot[j] * PAGE, cache_column), (PAGE, cache_width))
        for j in range(slots_here)
    ]
    cache_here = jnp.stack(pages, axis=0)
    return (attended, cache_here)


def solution(mesh):
    seq_size, tp_size = mesh.devices.shape
    split_mesh = jax.sharding.Mesh(
        mesh.devices.reshape(seq_size, tp_size // 2, 2), ("seq", "tpz", "tpx")
    )
    tp = ("tpz", "tpx")
    placed = (P("seq", None), P(), P(None, tp), P(), P(), P(tp, None), P(), P())
    return jax.shard_map(
        on_device,
        mesh=split_mesh,
        in_specs=placed,
        out_specs=(P(("seq",) + tp, None), P("seq", None, tp)),
        check_vma=False,
    )
```

```python
import functools

import jax
import jax.numpy as jnp
from jax import lax
from jax.experimental import pallas as pl
from jax.experimental.pallas import tpu as pltpu
from jax.sharding import PartitionSpec as P

HD = 128
PAGE = 128
BQ = 256
CHUNKS = 2
BK = 1024


epsilon = 1e-05
rope_base = 5000000.0


def segment_start(token_index, prompt_lengths):
    prompt_ends = jnp.cumsum(prompt_lengths)
    finished = prompt_ends[None, :] <= token_index[:, None]
    return jnp.sum(jnp.where(finished, prompt_lengths[None, :], 0), axis=1)


def rotate(vectors, position):
    half_size = HD // 2
    frequency = rope_base ** (-(2.0 * jnp.arange(half_size, dtype=jnp.float32)) / HD)
    angle = position.astype(jnp.float32)[:, None] * frequency[None, :]
    cosine = jnp.cos(angle)[:, None, :]
    sine = jnp.sin(angle)[:, None, :]
    first_half = vectors[..., :half_size]
    second_half = vectors[..., half_size:]
    return jnp.concatenate(
        [first_half * cosine - second_half * sine, second_half * cosine + first_half * sine],
        axis=-1,
    )


def normalize(tokens, norm_gain):
    hidden = tokens.astype(jnp.float32)
    factor = lax.rsqrt(jnp.mean(hidden * hidden, axis=-1, keepdims=True) + epsilon)
    return (hidden * factor * norm_gain.astype(jnp.float32)).astype(jnp.bfloat16)


def flash_kernel(lo_ref, hi_ref, base_ref, last_start_ref, q_ref, start_ref, index_ref, kv_ref, w_ref, o_ref):
    i = pl.program_id(0)
    heads = q_ref.shape[1] // HD
    row_index = index_ref[...]
    row_start = start_ref[...]
    scale = HD ** (-0.5)

    def step(kb, carry, masked):
        offset = pl.multiple_of(kb * BK, BK)
        keys = kv_ref[pl.ds(offset, BK), pl.ds(0, HD)]
        values = kv_ref[pl.ds(offset, BK), pl.ds(HD, HD)]
        values_ones = jnp.concatenate([values, jnp.ones((BK, HD), values.dtype)], axis=1)
        if masked:
            key_index = offset + lax.broadcasted_iota(jnp.int32, (1, BK), 1)
            visible = (key_index >= row_start) & (key_index <= row_index)
        updated = []
        for h in range(heads):
            running_max, running_sum, weighted = carry[h]
            q = q_ref[:, pl.ds(h * HD, HD)]
            scores = lax.dot_general(
                q, keys, (((1,), (1,)), ((), ())), preferred_element_type=jnp.float32
            ) * scale
            if masked:
                scores = jnp.where(visible, scores, -1e30)
            fresh_max = jnp.maximum(running_max, jnp.max(scores, axis=1, keepdims=True))
            weights = jnp.exp(scores - fresh_max)
            if masked:
                weights = jnp.where(visible, weights, 0.0)
            shrink = jnp.exp(running_max - fresh_max)
            both = jnp.dot(
                weights.astype(jnp.bfloat16), values_ones, preferred_element_type=jnp.float32
            )
            running_sum = running_sum * shrink + both[:, HD:]
            weighted = weighted * shrink + both[:, :HD]
            updated.append((fresh_max, running_sum, weighted))
        return tuple(updated)

    lo = lo_ref[i]
    hi = hi_ref[i] + 1
    full_lo = (last_start_ref[i] + BK - 1) // BK
    full_hi = (base_ref[i] + 1) // BK
    mid_lo = jnp.minimum(jnp.maximum(full_lo, lo), hi)
    mid_hi = jnp.maximum(mid_lo, jnp.minimum(full_hi, hi))
    carry = tuple(
        (
            jnp.full((BQ, 1), -1e30, jnp.float32),
            jnp.zeros((BQ, HD), jnp.float32),
            jnp.zeros((BQ, HD), jnp.float32),
        )
        for h in range(heads)
    )
    before = mid_lo - lo

    def masked_step(j, carry):
        kb = jnp.where(j < before, lo + j, mid_hi + j - before)
        return step(kb, carry, masked=True)

    carry = lax.fori_loop(0, before + hi - mid_hi, masked_step, carry)
    carry = lax.fori_loop(mid_lo, mid_hi, functools.partial(step, masked=False), carry)
    heads_out = jnp.concatenate(
        [(weighted / running_sum).astype(jnp.bfloat16) for _, running_sum, weighted in carry],
        axis=1,
    )
    tile = 512
    for n in range(o_ref.shape[1] // tile):
        o_ref[:, pl.ds(n * tile, tile)] = jnp.dot(
            heads_out, w_ref[:, pl.ds(n * tile, tile)], preferred_element_type=jnp.float32
        ).astype(o_ref.dtype)


def flash_attention(queries, row_start, row_index, key_values, w_out, bounds):
    rows, width = queries.shape
    q_blocks = rows // BQ
    kv_rows = key_values.shape[0]
    model_width = w_out.shape[1]
    rows_of = lambda i, *_: (i, 0)
    grid_spec = pltpu.PrefetchScalarGridSpec(
        num_scalar_prefetch=4,
        grid=(q_blocks,),
        in_specs=[
            pl.BlockSpec((BQ, width), rows_of),
            pl.BlockSpec((BQ, 1), rows_of),
            pl.BlockSpec((BQ, 1), rows_of),
            pl.BlockSpec((kv_rows, 2 * HD), lambda i, *_: (0, 0)),
            pl.BlockSpec((width, model_width), lambda i, *_: (0, 0)),
        ],
        out_specs=pl.BlockSpec((BQ, model_width), rows_of),
    )
    return pl.pallas_call(
        flash_kernel,
        grid_spec=grid_spec,
        out_shape=jax.ShapeDtypeStruct((rows, model_width), jnp.bfloat16),
    )(*bounds, queries, row_start, row_index, key_values, w_out)


def on_device(tokens, norm_gain, w_query, w_key, w_value, w_out, prompt_lengths, page_slots):
    row_count = tokens.shape[0]
    tp_count = lax.axis_size("tpz") * lax.axis_size("tpx")
    seq_rank = lax.axis_index("seq")
    tp_rank = lax.axis_index("tpz") * lax.axis_size("tpx") + lax.axis_index("tpx")
    heads_here = w_query.shape[1] // HD
    kv_heads = w_key.shape[1] // HD
    sharing = tp_count // kv_heads
    kv_head = tp_rank // sharing
    token_index = seq_rank * row_count + jnp.arange(row_count, dtype=jnp.int32)
    start = segment_start(token_index, prompt_lengths)
    position = token_index - start
    normed = normalize(tokens, norm_gain)

    key_columns = lax.dynamic_slice_in_dim(w_key, kv_head * HD, HD, 1)
    value_columns = lax.dynamic_slice_in_dim(w_value, kv_head * HD, HD, 1)
    keys_here = rotate(
        jnp.dot(normed, key_columns, preferred_element_type=jnp.float32)[:, None, :], position
    )[:, 0].astype(jnp.bfloat16)
    values_here = jnp.dot(normed, value_columns, preferred_element_type=jnp.float32).astype(
        jnp.bfloat16
    )
    keys_values = jnp.concatenate([keys_here, values_here], axis=1)
    gathered = lax.all_gather(keys_values, "seq", axis=0, tiled=True)

    queries = rotate(
        jnp.dot(normed, w_query, preferred_element_type=jnp.float32).reshape(
            row_count, heads_here, HD
        ),
        position,
    ).astype(jnp.bfloat16).reshape(row_count, heads_here * HD)

    piece = row_count // tp_count // CHUNKS
    chunk_queries = queries.reshape(tp_count, CHUNKS, piece, heads_here * HD)
    chunk_start = start.reshape(tp_count, CHUNKS, piece)
    chunk_index = token_index.reshape(tp_count, CHUNKS, piece)
    chunk_inputs = []
    for c in range(CHUNKS):
        q_rows = chunk_queries[:, c].reshape(tp_count * piece, heads_here * HD)
        s_rows = chunk_start[:, c].reshape(tp_count * piece)
        i_rows = chunk_index[:, c].reshape(tp_count * piece)
        bounds = (s_rows[:1] // BK, i_rows[-1:] // BK, i_rows[:1], s_rows[-1:])
        chunk_inputs.append((q_rows, s_rows[:, None], i_rows[:, None], bounds))
    chunk_inputs = lax.optimization_barrier(chunk_inputs)
    outputs = []
    for q_rows, s_rows, i_rows, bounds in chunk_inputs:
        partial_out = flash_attention(q_rows, s_rows, i_rows, gathered, w_out, bounds)
        received = lax.all_to_all(
            partial_out, ("tpz", "tpx"), split_axis=0, concat_axis=0, tiled=True
        ).reshape(tp_count, piece, -1)
        summed = received[0].astype(jnp.float32)
        for t in range(1, tp_count):
            summed = summed + received[t].astype(jnp.float32)
        outputs.append(summed.astype(jnp.bfloat16))
    attended = jnp.stack(outputs, axis=0).reshape(-1, outputs[0].shape[1])

    cache_width = 2 * HD // sharing
    cache_column = tp_rank % sharing * cache_width
    slots_here = row_count // PAGE
    page_total = page_slots.shape[0]
    wanted = seq_rank * slots_here + jnp.arange(slots_here, dtype=jnp.int32)
    page_of_slot = jnp.sum(
        jnp.where(
            page_slots[None, :] == wanted[:, None],
            jnp.arange(page_total, dtype=jnp.int32)[None, :],
            0,
        ),
        axis=1,
    )
    pages = [
        lax.dynamic_slice(gathered, (page_of_slot[j] * PAGE, cache_column), (PAGE, cache_width))
        for j in range(slots_here)
    ]
    cache_here = jnp.stack(pages, axis=0)
    return (attended, cache_here)


def solution(mesh):
    seq_size, tp_size = mesh.devices.shape
    split_mesh = jax.sharding.Mesh(
        mesh.devices.reshape(seq_size, tp_size // 2, 2), ("seq", "tpz", "tpx")
    )
    tp = ("tpz", "tpx")
    placed = (P("seq", None), P(), P(None, tp), P(), P(), P(tp, None), P(), P())
    return jax.shard_map(
        on_device,
        mesh=split_mesh,
        in_specs=placed,
        out_specs=(P(("seq",) + tp, None), P("seq", None, tp)),
        check_vma=False,
    )
```

```python
import functools

import jax
import jax.numpy as jnp
from jax import lax
from jax.experimental import pallas as pl
from jax.experimental.pallas import tpu as pltpu
from jax.sharding import PartitionSpec as P

HD = 128
PAGE = 128
BK = 1024


epsilon = 1e-05
rope_base = 5000000.0


def segment_start(token_index, prompt_lengths):
    prompt_ends = jnp.cumsum(prompt_lengths)
    finished = prompt_ends[None, :] <= token_index[:, None]
    return jnp.sum(jnp.where(finished, prompt_lengths[None, :], 0), axis=1)


def rotate(vectors, position):
    half_size = HD // 2
    frequency = rope_base ** (-(2.0 * jnp.arange(half_size, dtype=jnp.float32)) / HD)
    angle = position.astype(jnp.float32)[:, None] * frequency[None, :]
    cosine = jnp.cos(angle)[:, None, :]
    sine = jnp.sin(angle)[:, None, :]
    first_half = vectors[..., :half_size]
    second_half = vectors[..., half_size:]
    return jnp.concatenate(
        [first_half * cosine - second_half * sine, second_half * cosine + first_half * sine],
        axis=-1,
    )


def normalize(tokens, norm_gain):
    hidden = tokens.astype(jnp.float32)
    factor = lax.rsqrt(jnp.mean(hidden * hidden, axis=-1, keepdims=True) + epsilon)
    return (hidden * factor * norm_gain.astype(jnp.float32)).astype(jnp.bfloat16)


def flash_kernel(lo_ref, hi_ref, base_ref, last_start_ref, q_ref, start_ref, index_ref, kv_ref, w_ref, o_ref):
    i = pl.program_id(0)
    heads = q_ref.shape[1] // HD
    block_rows = q_ref.shape[0]
    row_index = index_ref[...]
    row_start = start_ref[...]
    scale = HD ** (-0.5)

    def step(kb, carry, masked):
        offset = pl.multiple_of(kb * BK, BK)
        keys = kv_ref[pl.ds(offset, BK), pl.ds(0, HD)]
        values = kv_ref[pl.ds(offset, BK), pl.ds(HD, HD)]
        values_ones = jnp.concatenate([values, jnp.ones((BK, HD), values.dtype)], axis=1)
        if masked:
            key_index = offset + lax.broadcasted_iota(jnp.int32, (1, BK), 1)
            visible = (key_index >= row_start) & (key_index <= row_index)
        updated = []
        for h in range(heads):
            running_max, running_sum, weighted = carry[h]
            q = q_ref[:, pl.ds(h * HD, HD)]
            scores = lax.dot_general(
                q, keys, (((1,), (1,)), ((), ())), preferred_element_type=jnp.float32
            ) * scale
            if masked:
                scores = jnp.where(visible, scores, -1e30)
            fresh_max = jnp.maximum(running_max, jnp.max(scores, axis=1, keepdims=True))
            weights = jnp.exp(scores - fresh_max)
            if masked:
                weights = jnp.where(visible, weights, 0.0)
            shrink = jnp.exp(running_max - fresh_max)
            both = jnp.dot(
                weights.astype(jnp.bfloat16), values_ones, preferred_element_type=jnp.float32
            )
            running_sum = running_sum * shrink + both[:, HD:]
            weighted = weighted * shrink + both[:, :HD]
            updated.append((fresh_max, running_sum, weighted))
        return tuple(updated)

    lo = lo_ref[i]
    hi = hi_ref[i] + 1
    full_lo = (last_start_ref[i] + BK - 1) // BK
    full_hi = (base_ref[i] + 1) // BK
    mid_lo = jnp.minimum(jnp.maximum(full_lo, lo), hi)
    mid_hi = jnp.maximum(mid_lo, jnp.minimum(full_hi, hi))
    carry = tuple(
        (
            jnp.full((block_rows, 1), -1e30, jnp.float32),
            jnp.zeros((block_rows, HD), jnp.float32),
            jnp.zeros((block_rows, HD), jnp.float32),
        )
        for h in range(heads)
    )
    before = mid_lo - lo

    def masked_step(j, carry):
        kb = jnp.where(j < before, lo + j, mid_hi + j - before)
        return step(kb, carry, masked=True)

    carry = lax.fori_loop(0, before + hi - mid_hi, masked_step, carry)
    carry = lax.fori_loop(mid_lo, mid_hi, functools.partial(step, masked=False), carry)
    heads_out = jnp.concatenate(
        [(weighted / running_sum).astype(jnp.bfloat16) for _, running_sum, weighted in carry],
        axis=1,
    )
    tile = 512
    for n in range(o_ref.shape[1] // tile):
        o_ref[:, pl.ds(n * tile, tile)] = jnp.dot(
            heads_out, w_ref[:, pl.ds(n * tile, tile)], preferred_element_type=jnp.float32
        ).astype(o_ref.dtype)


def flash_attention(queries, row_start, row_index, key_values, w_out, bounds):
    rows, width = queries.shape
    q_blocks = 1
    block_rows = rows
    kv_rows = key_values.shape[0]
    model_width = w_out.shape[1]
    rows_of = lambda i, *_: (i, 0)
    grid_spec = pltpu.PrefetchScalarGridSpec(
        num_scalar_prefetch=4,
        grid=(q_blocks,),
        in_specs=[
            pl.BlockSpec((block_rows, width), rows_of),
            pl.BlockSpec((block_rows, 1), rows_of),
            pl.BlockSpec((block_rows, 1), rows_of),
            pl.BlockSpec((kv_rows, 2 * HD), lambda i, *_: (0, 0)),
            pl.BlockSpec((width, model_width), lambda i, *_: (0, 0)),
        ],
        out_specs=pl.BlockSpec((block_rows, model_width), rows_of),
    )
    return pl.pallas_call(
        flash_kernel,
        grid_spec=grid_spec,
        out_shape=jax.ShapeDtypeStruct((rows, model_width), jnp.bfloat16),
    )(*bounds, queries, row_start, row_index, key_values, w_out)


def on_device(tokens, norm_gain, w_query, w_key, w_value, w_out, prompt_lengths, page_slots):
    row_count = tokens.shape[0]
    tp_count = lax.axis_size("tpz") * lax.axis_size("tpx")
    seq_rank = lax.axis_index("seq")
    tp_rank = lax.axis_index("tpz") * lax.axis_size("tpx") + lax.axis_index("tpx")
    heads_here = w_query.shape[1] // HD
    kv_heads = w_key.shape[1] // HD
    sharing = tp_count // kv_heads
    kv_head = tp_rank // sharing
    token_index = seq_rank * row_count + jnp.arange(row_count, dtype=jnp.int32)
    start = segment_start(token_index, prompt_lengths)
    position = token_index - start
    normed = normalize(tokens, norm_gain)

    key_columns = lax.dynamic_slice_in_dim(w_key, kv_head * HD, HD, 1)
    value_columns = lax.dynamic_slice_in_dim(w_value, kv_head * HD, HD, 1)
    keys_here = rotate(
        jnp.dot(normed, key_columns, preferred_element_type=jnp.float32)[:, None, :], position
    )[:, 0].astype(jnp.bfloat16)
    values_here = jnp.dot(normed, value_columns, preferred_element_type=jnp.float32).astype(
        jnp.bfloat16
    )
    keys_values = jnp.concatenate([keys_here, values_here], axis=1)
    gathered = lax.all_gather(keys_values, "seq", axis=0, tiled=True)

    queries = rotate(
        jnp.dot(normed, w_query, preferred_element_type=jnp.float32).reshape(
            row_count, heads_here, HD
        ),
        position,
    ).astype(jnp.bfloat16).reshape(row_count, heads_here * HD)

    owned = row_count // tp_count
    split = owned * 5 // 8
    parts = ((0, split), (split, owned))
    owned_queries = queries.reshape(tp_count, owned, heads_here * HD)
    owned_start = start.reshape(tp_count, owned)
    owned_index = token_index.reshape(tp_count, owned)
    chunk_inputs = []
    for first, last in parts:
        piece = last - first
        q_rows = owned_queries[:, first:last].reshape(tp_count * piece, heads_here * HD)
        s_rows = owned_start[:, first:last].reshape(tp_count * piece)
        i_rows = owned_index[:, first:last].reshape(tp_count * piece)
        bounds = (s_rows[:1] // BK, i_rows[-1:] // BK, i_rows[:1], s_rows[-1:])
        chunk_inputs.append((q_rows, s_rows[:, None], i_rows[:, None], bounds))
    chunk_inputs = lax.optimization_barrier(chunk_inputs)
    outputs = []
    for q_rows, s_rows, i_rows, bounds in chunk_inputs:
        partial_out = flash_attention(q_rows, s_rows, i_rows, gathered, w_out, bounds)
        received = lax.all_to_all(
            partial_out, ("tpz", "tpx"), split_axis=0, concat_axis=0, tiled=True
        ).reshape(tp_count, q_rows.shape[0] // tp_count, -1)
        summed = received[0].astype(jnp.float32)
        for t in range(1, tp_count):
            summed = summed + received[t].astype(jnp.float32)
        outputs.append(summed.astype(jnp.bfloat16))
    attended = jnp.concatenate(outputs, axis=0)

    cache_width = 2 * HD // sharing
    cache_column = tp_rank % sharing * cache_width
    slots_here = row_count // PAGE
    page_total = page_slots.shape[0]
    wanted = seq_rank * slots_here + jnp.arange(slots_here, dtype=jnp.int32)
    page_of_slot = jnp.sum(
        jnp.where(
            page_slots[None, :] == wanted[:, None],
            jnp.arange(page_total, dtype=jnp.int32)[None, :],
            0,
        ),
        axis=1,
    )
    pages = [
        lax.dynamic_slice(gathered, (page_of_slot[j] * PAGE, cache_column), (PAGE, cache_width))
        for j in range(slots_here)
    ]
    cache_here = jnp.stack(pages, axis=0)
    return (attended, cache_here)


def solution(mesh):
    seq_size, tp_size = mesh.devices.shape
    split_mesh = jax.sharding.Mesh(
        mesh.devices.reshape(seq_size, tp_size // 2, 2), ("seq", "tpz", "tpx")
    )
    tp = ("tpz", "tpx")
    placed = (P("seq", None), P(), P(None, tp), P(), P(), P(tp, None), P(), P())
    return jax.shard_map(
        on_device,
        mesh=split_mesh,
        in_specs=placed,
        out_specs=(P(("seq",) + tp, None), P("seq", None, tp)),
        check_vma=False,
    )
```

```python
import functools

import jax
import jax.numpy as jnp
from jax import lax
from jax.experimental import pallas as pl
from jax.experimental.pallas import tpu as pltpu
from jax.sharding import PartitionSpec as P

HD = 128
PAGE = 128
BK = 1024


epsilon = 1e-05
rope_base = 5000000.0


def segment_start(token_index, prompt_lengths):
    prompt_ends = jnp.cumsum(prompt_lengths)
    finished = prompt_ends[None, :] <= token_index[:, None]
    return jnp.sum(jnp.where(finished, prompt_lengths[None, :], 0), axis=1)


def rotate(vectors, position):
    half_size = HD // 2
    frequency = rope_base ** (-(2.0 * jnp.arange(half_size, dtype=jnp.float32)) / HD)
    angle = position.astype(jnp.float32)[:, None] * frequency[None, :]
    cosine = jnp.cos(angle)[:, None, :]
    sine = jnp.sin(angle)[:, None, :]
    first_half = vectors[..., :half_size]
    second_half = vectors[..., half_size:]
    return jnp.concatenate(
        [first_half * cosine - second_half * sine, second_half * cosine + first_half * sine],
        axis=-1,
    )


def normalize(tokens, norm_gain):
    hidden = tokens.astype(jnp.float32)
    factor = lax.rsqrt(jnp.mean(hidden * hidden, axis=-1, keepdims=True) + epsilon)
    return (hidden * factor * norm_gain.astype(jnp.float32)).astype(jnp.bfloat16)


def flash_kernel(lo_ref, hi_ref, base_ref, last_start_ref, q_ref, start_ref, index_ref, kv_ref, w_ref, o_ref):
    i = pl.program_id(0)
    heads = q_ref.shape[1] // HD
    block_rows = q_ref.shape[0]
    row_index = index_ref[...]
    row_start = start_ref[...]
    scale = HD ** (-0.5)

    def step(kb, carry, masked):
        offset = pl.multiple_of(kb * BK, BK)
        keys = kv_ref[pl.ds(offset, BK), pl.ds(0, HD)]
        values = kv_ref[pl.ds(offset, BK), pl.ds(HD, HD)]
        values_ones = jnp.concatenate([values, jnp.ones((BK, HD), values.dtype)], axis=1)
        if masked:
            key_index = offset + lax.broadcasted_iota(jnp.int32, (1, BK), 1)
            visible = (key_index >= row_start) & (key_index <= row_index)
        updated = []
        for h in range(heads):
            running_max, running_sum, weighted = carry[h]
            q = q_ref[:, pl.ds(h * HD, HD)]
            scores = lax.dot_general(
                q, keys, (((1,), (1,)), ((), ())), preferred_element_type=jnp.float32
            ) * scale
            if masked:
                scores = jnp.where(visible, scores, -1e30)
            fresh_max = jnp.maximum(running_max, jnp.max(scores, axis=1, keepdims=True))
            weights = jnp.exp(scores - fresh_max)
            if masked:
                weights = jnp.where(visible, weights, 0.0)
            shrink = jnp.exp(running_max - fresh_max)
            both = jnp.dot(
                weights.astype(jnp.bfloat16), values_ones, preferred_element_type=jnp.float32
            )
            running_sum = running_sum * shrink + both[:, HD:]
            weighted = weighted * shrink + both[:, :HD]
            updated.append((fresh_max, running_sum, weighted))
        return tuple(updated)

    lo = lo_ref[i]
    hi = hi_ref[i] + 1
    full_lo = (last_start_ref[i] + BK - 1) // BK
    full_hi = (base_ref[i] + 1) // BK
    mid_lo = jnp.minimum(jnp.maximum(full_lo, lo), hi)
    mid_hi = jnp.maximum(mid_lo, jnp.minimum(full_hi, hi))
    carry = tuple(
        (
            jnp.full((block_rows, 1), -1e30, jnp.float32),
            jnp.zeros((block_rows, HD), jnp.float32),
            jnp.zeros((block_rows, HD), jnp.float32),
        )
        for h in range(heads)
    )
    before = mid_lo - lo

    def masked_step(j, carry):
        kb = jnp.where(j < before, lo + j, mid_hi + j - before)
        return step(kb, carry, masked=True)

    carry = lax.fori_loop(0, before + hi - mid_hi, masked_step, carry)
    carry = lax.fori_loop(mid_lo, mid_hi, functools.partial(step, masked=False), carry)
    heads_out = jnp.concatenate(
        [(weighted / running_sum).astype(jnp.bfloat16) for _, running_sum, weighted in carry],
        axis=1,
    )
    tile = 512
    for n in range(o_ref.shape[1] // tile):
        o_ref[:, pl.ds(n * tile, tile)] = jnp.dot(
            heads_out, w_ref[:, pl.ds(n * tile, tile)], preferred_element_type=jnp.float32
        ).astype(o_ref.dtype)


def flash_attention(queries, row_start, row_index, key_values, w_out, bounds):
    rows, width = queries.shape
    q_blocks = 1
    block_rows = rows
    kv_rows = key_values.shape[0]
    model_width = w_out.shape[1]
    rows_of = lambda i, *_: (i, 0)
    grid_spec = pltpu.PrefetchScalarGridSpec(
        num_scalar_prefetch=4,
        grid=(q_blocks,),
        in_specs=[
            pl.BlockSpec((block_rows, width), rows_of),
            pl.BlockSpec((block_rows, 1), rows_of),
            pl.BlockSpec((block_rows, 1), rows_of),
            pl.BlockSpec((kv_rows, 2 * HD), lambda i, *_: (0, 0)),
            pl.BlockSpec((width, model_width), lambda i, *_: (0, 0)),
        ],
        out_specs=pl.BlockSpec((block_rows, model_width), rows_of),
    )
    return pl.pallas_call(
        flash_kernel,
        grid_spec=grid_spec,
        out_shape=jax.ShapeDtypeStruct((rows, model_width), jnp.bfloat16),
    )(*bounds, queries, row_start, row_index, key_values, w_out)


def on_device(tokens, norm_gain, w_query, w_key, w_value, w_out, prompt_lengths, page_slots):
    row_count = tokens.shape[0]
    tp_count = lax.axis_size("tpz") * lax.axis_size("tpx")
    seq_rank = lax.axis_index("seq")
    tp_rank = lax.axis_index("tpz") * lax.axis_size("tpx") + lax.axis_index("tpx")
    heads_here = w_query.shape[1] // HD
    kv_heads = w_key.shape[1] // HD
    sharing = tp_count // kv_heads
    kv_head = tp_rank // sharing
    token_index = seq_rank * row_count + jnp.arange(row_count, dtype=jnp.int32)
    start = segment_start(token_index, prompt_lengths)
    position = token_index - start
    normed = normalize(tokens, norm_gain)

    key_columns = lax.dynamic_slice_in_dim(w_key, kv_head * HD, HD, 1)
    value_columns = lax.dynamic_slice_in_dim(w_value, kv_head * HD, HD, 1)
    keys_here = rotate(
        jnp.dot(normed, key_columns, preferred_element_type=jnp.float32)[:, None, :], position
    )[:, 0].astype(jnp.bfloat16)
    values_here = jnp.dot(normed, value_columns, preferred_element_type=jnp.float32).astype(
        jnp.bfloat16
    )
    keys_values = jnp.concatenate([keys_here, values_here], axis=1)
    gathered = lax.all_gather(keys_values, "seq", axis=0, tiled=True)

    queries = rotate(
        jnp.dot(normed, w_query, preferred_element_type=jnp.float32).reshape(
            row_count, heads_here, HD
        ),
        position,
    ).astype(jnp.bfloat16).reshape(row_count, heads_here * HD)

    owned = row_count // tp_count
    split = owned * 5 // 8
    parts = ((0, split), (split, owned))
    owned_queries = queries.reshape(tp_count, owned, heads_here * HD)
    owned_start = start.reshape(tp_count, owned)
    owned_index = token_index.reshape(tp_count, owned)
    chunk_inputs = []
    for first, last in parts:
        piece = last - first
        q_rows = owned_queries[:, first:last].reshape(tp_count * piece, heads_here * HD)
        s_rows = owned_start[:, first:last].reshape(tp_count * piece)
        i_rows = owned_index[:, first:last].reshape(tp_count * piece)
        bounds = (s_rows[:1] // BK, i_rows[-1:] // BK, i_rows[:1], s_rows[-1:])
        chunk_inputs.append((q_rows, s_rows[:, None], i_rows[:, None], bounds))
    chunk_inputs = lax.optimization_barrier(chunk_inputs)
    outputs = []
    previous = None
    for inputs in chunk_inputs:
        if previous is not None:
            previous, inputs = lax.optimization_barrier((previous, inputs))
        q_rows, s_rows, i_rows, bounds = inputs
        partial_out = flash_attention(q_rows, s_rows, i_rows, gathered, w_out, bounds)
        previous = partial_out
        received = lax.all_to_all(
            partial_out, ("tpz", "tpx"), split_axis=0, concat_axis=0, tiled=True
        ).reshape(tp_count, q_rows.shape[0] // tp_count, -1)
        summed = received[0].astype(jnp.float32)
        for t in range(1, tp_count):
            summed = summed + received[t].astype(jnp.float32)
        outputs.append(summed.astype(jnp.bfloat16))
    attended = jnp.concatenate(outputs, axis=0)

    cache_width = 2 * HD // sharing
    cache_column = tp_rank % sharing * cache_width
    slots_here = row_count // PAGE
    page_total = page_slots.shape[0]
    wanted = seq_rank * slots_here + jnp.arange(slots_here, dtype=jnp.int32)
    page_of_slot = jnp.sum(
        jnp.where(
            page_slots[None, :] == wanted[:, None],
            jnp.arange(page_total, dtype=jnp.int32)[None, :],
            0,
        ),
        axis=1,
    )
    pages = [
        lax.dynamic_slice(gathered, (page_of_slot[j] * PAGE, cache_column), (PAGE, cache_width))
        for j in range(slots_here)
    ]
    cache_here = jnp.stack(pages, axis=0)
    return (attended, cache_here)


def solution(mesh):
    seq_size, tp_size = mesh.devices.shape
    split_mesh = jax.sharding.Mesh(
        mesh.devices.reshape(seq_size, tp_size // 2, 2), ("seq", "tpz", "tpx")
    )
    tp = ("tpz", "tpx")
    placed = (P("seq", None), P(), P(None, tp), P(), P(), P(tp, None), P(), P())
    return jax.shard_map(
        on_device,
        mesh=split_mesh,
        in_specs=placed,
        out_specs=(P(("seq",) + tp, None), P("seq", None, tp)),
        check_vma=False,
    )
```

```python
import functools

import jax
import jax.numpy as jnp
from jax import lax
from jax.experimental import pallas as pl
from jax.experimental.pallas import tpu as pltpu
from jax.sharding import PartitionSpec as P

HD = 128
PAGE = 128
BQ = 256
CHUNKS = 2
BK = 1024


epsilon = 1e-05
rope_base = 5000000.0


def segment_start(token_index, prompt_lengths):
    prompt_ends = jnp.cumsum(prompt_lengths)
    finished = prompt_ends[None, :] <= token_index[:, None]
    return jnp.sum(jnp.where(finished, prompt_lengths[None, :], 0), axis=1)


def rotate(vectors, position):
    half_size = HD // 2
    frequency = rope_base ** (-(2.0 * jnp.arange(half_size, dtype=jnp.float32)) / HD)
    angle = position.astype(jnp.float32)[:, None] * frequency[None, :]
    cosine = jnp.cos(angle)[:, None, :]
    sine = jnp.sin(angle)[:, None, :]
    first_half = vectors[..., :half_size]
    second_half = vectors[..., half_size:]
    return jnp.concatenate(
        [first_half * cosine - second_half * sine, second_half * cosine + first_half * sine],
        axis=-1,
    )


def normalize(tokens, norm_gain):
    hidden = tokens.astype(jnp.float32)
    factor = lax.rsqrt(jnp.mean(hidden * hidden, axis=-1, keepdims=True) + epsilon)
    return (hidden * factor * norm_gain.astype(jnp.float32)).astype(jnp.bfloat16)


def flash_kernel(lo_ref, hi_ref, base_ref, last_start_ref, q_ref, start_ref, index_ref, kv_ref, w_ref, o_ref):
    i = pl.program_id(0)
    heads = q_ref.shape[1] // HD
    row_index = index_ref[...]
    row_start = start_ref[...]
    scale = HD ** (-0.5)

    def step(kb, carry, masked):
        offset = pl.multiple_of(kb * BK, BK)
        keys = kv_ref[pl.ds(offset, BK), pl.ds(0, HD)]
        values = kv_ref[pl.ds(offset, BK), pl.ds(HD, HD)]
        values_ones = jnp.concatenate([values, jnp.ones((BK, HD), values.dtype)], axis=1)
        if masked:
            key_index = offset + lax.broadcasted_iota(jnp.int32, (1, BK), 1)
            visible = (key_index >= row_start) & (key_index <= row_index)
        updated = []
        for h in range(heads):
            running_max, running_sum, weighted = carry[h]
            q = q_ref[:, pl.ds(h * HD, HD)]
            scores = lax.dot_general(
                q, keys, (((1,), (1,)), ((), ())), preferred_element_type=jnp.float32
            ) * scale
            if masked:
                scores = jnp.where(visible, scores, -1e30)
            fresh_max = jnp.maximum(running_max, jnp.max(scores, axis=1, keepdims=True))
            weights = jnp.exp(scores - fresh_max)
            if masked:
                weights = jnp.where(visible, weights, 0.0)
            shrink = jnp.exp(running_max - fresh_max)
            both = jnp.dot(
                weights.astype(jnp.bfloat16), values_ones, preferred_element_type=jnp.float32
            )
            running_sum = running_sum * shrink + both[:, HD:]
            weighted = weighted * shrink + both[:, :HD]
            updated.append((fresh_max, running_sum, weighted))
        return tuple(updated)

    lo = lo_ref[i]
    hi = hi_ref[i] + 1
    full_lo = (last_start_ref[i] + BK - 1) // BK
    full_hi = (base_ref[i] + 1) // BK
    mid_lo = jnp.minimum(jnp.maximum(full_lo, lo), hi)
    mid_hi = jnp.maximum(mid_lo, jnp.minimum(full_hi, hi))
    carry = tuple(
        (
            jnp.full((BQ, 1), -1e30, jnp.float32),
            jnp.zeros((BQ, HD), jnp.float32),
            jnp.zeros((BQ, HD), jnp.float32),
        )
        for h in range(heads)
    )
    before = mid_lo - lo

    def masked_step(j, carry):
        kb = jnp.where(j < before, lo + j, mid_hi + j - before)
        return step(kb, carry, masked=True)

    carry = lax.fori_loop(0, before + hi - mid_hi, masked_step, carry)
    carry = lax.fori_loop(mid_lo, mid_hi, functools.partial(step, masked=False), carry)
    heads_out = jnp.concatenate(
        [(weighted / running_sum).astype(jnp.bfloat16) for _, running_sum, weighted in carry],
        axis=1,
    )
    tile = 512
    for n in range(o_ref.shape[1] // tile):
        o_ref[:, pl.ds(n * tile, tile)] = jnp.dot(
            heads_out, w_ref[:, pl.ds(n * tile, tile)], preferred_element_type=jnp.float32
        ).astype(o_ref.dtype)


def flash_attention(queries, row_start, row_index, key_values, w_out, bounds):
    rows, width = queries.shape
    q_blocks = rows // BQ
    kv_rows = key_values.shape[0]
    model_width = w_out.shape[1]
    rows_of = lambda i, *_: (i, 0)
    grid_spec = pltpu.PrefetchScalarGridSpec(
        num_scalar_prefetch=4,
        grid=(q_blocks,),
        in_specs=[
            pl.BlockSpec((BQ, width), rows_of),
            pl.BlockSpec((BQ, 1), rows_of),
            pl.BlockSpec((BQ, 1), rows_of),
            pl.BlockSpec((kv_rows, 2 * HD), lambda i, *_: (0, 0)),
            pl.BlockSpec((width, model_width), lambda i, *_: (0, 0)),
        ],
        out_specs=pl.BlockSpec((BQ, model_width), rows_of),
    )
    return pl.pallas_call(
        flash_kernel,
        grid_spec=grid_spec,
        out_shape=jax.ShapeDtypeStruct((rows, model_width), jnp.bfloat16),
    )(*bounds, queries, row_start, row_index, key_values, w_out)


def on_device(tokens, norm_gain, w_query, w_key, w_value, w_out, prompt_lengths, page_slots):
    row_count = tokens.shape[0]
    tp_count = lax.axis_size("tpz") * lax.axis_size("tpx")
    seq_rank = lax.axis_index("seq")
    tp_rank = lax.axis_index("tpz") * lax.axis_size("tpx") + lax.axis_index("tpx")
    heads_here = w_query.shape[1] // HD
    kv_heads = w_key.shape[1] // HD
    sharing = tp_count // kv_heads
    kv_head = tp_rank // sharing
    token_index = seq_rank * row_count + jnp.arange(row_count, dtype=jnp.int32)
    start = segment_start(token_index, prompt_lengths)
    position = token_index - start
    normed = normalize(tokens, norm_gain)

    key_columns = lax.dynamic_slice_in_dim(w_key, kv_head * HD, HD, 1)
    value_columns = lax.dynamic_slice_in_dim(w_value, kv_head * HD, HD, 1)
    projected = jnp.dot(
        normed,
        jnp.concatenate([key_columns, value_columns], axis=1),
        preferred_element_type=jnp.float32,
    )
    keys_here = rotate(projected[:, None, :HD], position)[:, 0].astype(jnp.bfloat16)
    values_here = projected[:, HD:].astype(jnp.bfloat16)
    keys_values = jnp.concatenate([keys_here, values_here], axis=1)
    gathered = lax.all_gather(keys_values, "seq", axis=0, tiled=True)

    queries = rotate(
        jnp.dot(normed, w_query, preferred_element_type=jnp.float32).reshape(
            row_count, heads_here, HD
        ),
        position,
    ).astype(jnp.bfloat16).reshape(row_count, heads_here * HD)

    piece = row_count // tp_count // CHUNKS
    chunk_queries = queries.reshape(tp_count, CHUNKS, piece, heads_here * HD)
    chunk_start = start.reshape(tp_count, CHUNKS, piece)
    chunk_index = token_index.reshape(tp_count, CHUNKS, piece)
    chunk_inputs = []
    for c in range(CHUNKS):
        q_rows = chunk_queries[:, c].reshape(tp_count * piece, heads_here * HD)
        s_rows = chunk_start[:, c].reshape(tp_count * piece)
        i_rows = chunk_index[:, c].reshape(tp_count * piece)
        bounds = (s_rows[:1] // BK, i_rows[-1:] // BK, i_rows[:1], s_rows[-1:])
        chunk_inputs.append((q_rows, s_rows[:, None], i_rows[:, None], bounds))
    chunk_inputs = lax.optimization_barrier(chunk_inputs)
    outputs = []
    for q_rows, s_rows, i_rows, bounds in chunk_inputs:
        partial_out = flash_attention(q_rows, s_rows, i_rows, gathered, w_out, bounds)
        received = lax.all_to_all(
            partial_out, ("tpz", "tpx"), split_axis=0, concat_axis=0, tiled=True
        ).reshape(tp_count, piece, -1)
        summed = received[0].astype(jnp.float32)
        for t in range(1, tp_count):
            summed = summed + received[t].astype(jnp.float32)
        outputs.append(summed.astype(jnp.bfloat16))
    attended = jnp.stack(outputs, axis=0).reshape(-1, outputs[0].shape[1])

    cache_width = 2 * HD // sharing
    cache_column = tp_rank % sharing * cache_width
    slots_here = row_count // PAGE
    page_total = page_slots.shape[0]
    wanted = seq_rank * slots_here + jnp.arange(slots_here, dtype=jnp.int32)
    page_of_slot = jnp.sum(
        jnp.where(
            page_slots[None, :] == wanted[:, None],
            jnp.arange(page_total, dtype=jnp.int32)[None, :],
            0,
        ),
        axis=1,
    )
    pages = [
        lax.dynamic_slice(gathered, (page_of_slot[j] * PAGE, cache_column), (PAGE, cache_width))
        for j in range(slots_here)
    ]
    cache_here = jnp.stack(pages, axis=0)
    return (attended, cache_here)


def solution(mesh):
    seq_size, tp_size = mesh.devices.shape
    split_mesh = jax.sharding.Mesh(
        mesh.devices.reshape(seq_size, tp_size // 2, 2), ("seq", "tpz", "tpx")
    )
    tp = ("tpz", "tpx")
    placed = (P("seq", None), P(), P(None, tp), P(), P(), P(tp, None), P(), P())
    return jax.shard_map(
        on_device,
        mesh=split_mesh,
        in_specs=placed,
        out_specs=(P(("seq",) + tp, None), P("seq", None, tp)),
        check_vma=False,
    )
```

```python
import functools

import jax
import jax.numpy as jnp
from jax import lax
from jax.experimental import pallas as pl
from jax.experimental.pallas import tpu as pltpu
from jax.sharding import PartitionSpec as P

HD = 128
PAGE = 128
BQ = 256
CHUNKS = 2
BK = 1024


epsilon = 1e-05
rope_base = 5000000.0


def segment_start(token_index, prompt_lengths):
    prompt_ends = jnp.cumsum(prompt_lengths)
    finished = prompt_ends[None, :] <= token_index[:, None]
    return jnp.sum(jnp.where(finished, prompt_lengths[None, :], 0), axis=1)


def rotate(vectors, position):
    half_size = HD // 2
    frequency = rope_base ** (-(2.0 * jnp.arange(half_size, dtype=jnp.float32)) / HD)
    angle = position.astype(jnp.float32)[:, None] * frequency[None, :]
    cosine = jnp.cos(angle)[:, None, :]
    sine = jnp.sin(angle)[:, None, :]
    first_half = vectors[..., :half_size]
    second_half = vectors[..., half_size:]
    return jnp.concatenate(
        [first_half * cosine - second_half * sine, second_half * cosine + first_half * sine],
        axis=-1,
    )


def normalize(tokens, norm_gain):
    hidden = tokens.astype(jnp.float32)
    factor = lax.rsqrt(jnp.mean(hidden * hidden, axis=-1, keepdims=True) + epsilon)
    return (hidden * factor * norm_gain.astype(jnp.float32)).astype(jnp.bfloat16)


def flash_kernel(lo_ref, hi_ref, base_ref, last_start_ref, q_ref, start_ref, index_ref, kv_ref, w_ref, o_ref):
    i = pl.program_id(0)
    heads = q_ref.shape[1] // HD
    row_index = index_ref[:, 0:1]
    row_start = start_ref[:, 0:1]
    scale = HD ** (-0.5)

    def step(kb, carry, masked):
        offset = pl.multiple_of(kb * BK, BK)
        keys = kv_ref[pl.ds(offset, BK), pl.ds(0, HD)]
        values = kv_ref[pl.ds(offset, BK), pl.ds(HD, HD)]
        values_ones = jnp.concatenate([values, jnp.ones((BK, HD), values.dtype)], axis=1)
        if masked:
            key_index = offset + lax.broadcasted_iota(jnp.int32, (1, BK), 1)
            visible = (key_index >= row_start) & (key_index <= row_index)
        updated = []
        for h in range(heads):
            running_max, running_sum, weighted = carry[h]
            q = q_ref[:, pl.ds(h * HD, HD)]
            scores = lax.dot_general(
                q, keys, (((1,), (1,)), ((), ())), preferred_element_type=jnp.float32
            ) * scale
            if masked:
                scores = jnp.where(visible, scores, -1e30)
            fresh_max = jnp.maximum(running_max, jnp.max(scores, axis=1, keepdims=True))
            weights = jnp.exp(scores - fresh_max)
            if masked:
                weights = jnp.where(visible, weights, 0.0)
            shrink = jnp.exp(running_max - fresh_max)
            both = jnp.dot(
                weights.astype(jnp.bfloat16), values_ones, preferred_element_type=jnp.float32
            )
            running_sum = running_sum * shrink + both[:, HD:]
            weighted = weighted * shrink + both[:, :HD]
            updated.append((fresh_max, running_sum, weighted))
        return tuple(updated)

    lo = lo_ref[i]
    hi = hi_ref[i] + 1
    full_lo = (last_start_ref[i] + BK - 1) // BK
    full_hi = (base_ref[i] + 1) // BK
    mid_lo = jnp.minimum(jnp.maximum(full_lo, lo), hi)
    mid_hi = jnp.maximum(mid_lo, jnp.minimum(full_hi, hi))
    carry = tuple(
        (
            jnp.full((BQ, 1), -1e30, jnp.float32),
            jnp.zeros((BQ, HD), jnp.float32),
            jnp.zeros((BQ, HD), jnp.float32),
        )
        for h in range(heads)
    )
    before = mid_lo - lo

    def masked_step(j, carry):
        kb = jnp.where(j < before, lo + j, mid_hi + j - before)
        return step(kb, carry, masked=True)

    carry = lax.fori_loop(0, before + hi - mid_hi, masked_step, carry)
    carry = lax.fori_loop(mid_lo, mid_hi, functools.partial(step, masked=False), carry)
    heads_out = jnp.concatenate(
        [(weighted / running_sum).astype(jnp.bfloat16) for _, running_sum, weighted in carry],
        axis=1,
    )
    tile = 512
    for n in range(o_ref.shape[1] // tile):
        o_ref[:, pl.ds(n * tile, tile)] = jnp.dot(
            heads_out, w_ref[:, pl.ds(n * tile, tile)], preferred_element_type=jnp.float32
        ).astype(o_ref.dtype)


def flash_attention(queries, row_start, row_index, key_values, w_out, bounds):
    rows, width = queries.shape
    q_blocks = rows // BQ
    kv_rows = key_values.shape[0]
    model_width = w_out.shape[1]
    rows_of = lambda i, *_: (i, 0)
    grid_spec = pltpu.PrefetchScalarGridSpec(
        num_scalar_prefetch=4,
        grid=(q_blocks,),
        in_specs=[
            pl.BlockSpec((BQ, width), rows_of),
            pl.BlockSpec((BQ, HD), rows_of),
            pl.BlockSpec((BQ, HD), rows_of),
            pl.BlockSpec((kv_rows, 2 * HD), lambda i, *_: (0, 0)),
            pl.BlockSpec((width, model_width), lambda i, *_: (0, 0)),
        ],
        out_specs=pl.BlockSpec((BQ, model_width), rows_of),
    )
    return pl.pallas_call(
        flash_kernel,
        grid_spec=grid_spec,
        out_shape=jax.ShapeDtypeStruct((rows, model_width), jnp.bfloat16),
    )(*bounds, queries, row_start, row_index, key_values, w_out)


def on_device(tokens, norm_gain, w_query, w_key, w_value, w_out, prompt_lengths, page_slots):
    row_count = tokens.shape[0]
    tp_count = lax.axis_size("tpz") * lax.axis_size("tpx")
    seq_rank = lax.axis_index("seq")
    tp_rank = lax.axis_index("tpz") * lax.axis_size("tpx") + lax.axis_index("tpx")
    heads_here = w_query.shape[1] // HD
    kv_heads = w_key.shape[1] // HD
    sharing = tp_count // kv_heads
    kv_head = tp_rank // sharing
    token_index = seq_rank * row_count + jnp.arange(row_count, dtype=jnp.int32)
    start = segment_start(token_index, prompt_lengths)
    position = token_index - start
    normed = normalize(tokens, norm_gain)

    key_columns = lax.dynamic_slice_in_dim(w_key, kv_head * HD, HD, 1)
    value_columns = lax.dynamic_slice_in_dim(w_value, kv_head * HD, HD, 1)
    projected = jnp.dot(
        normed,
        jnp.concatenate([key_columns, value_columns], axis=1),
        preferred_element_type=jnp.float32,
    )
    keys_here = rotate(projected[:, None, :HD], position)[:, 0].astype(jnp.bfloat16)
    values_here = projected[:, HD:].astype(jnp.bfloat16)
    keys_values = jnp.concatenate([keys_here, values_here], axis=1)
    gathered = lax.all_gather(keys_values, "seq", axis=0, tiled=True)

    queries = rotate(
        jnp.dot(normed, w_query, preferred_element_type=jnp.float32).reshape(
            row_count, heads_here, HD
        ),
        position,
    ).astype(jnp.bfloat16).reshape(row_count, heads_here * HD)

    piece = row_count // tp_count // CHUNKS
    chunk_queries = queries.reshape(tp_count, CHUNKS, piece, heads_here * HD)
    chunk_start = start.reshape(tp_count, CHUNKS, piece)
    chunk_index = token_index.reshape(tp_count, CHUNKS, piece)
    chunk_inputs = []
    for c in range(CHUNKS):
        q_rows = chunk_queries[:, c].reshape(tp_count * piece, heads_here * HD)
        s_rows = chunk_start[:, c].reshape(tp_count * piece)
        i_rows = chunk_index[:, c].reshape(tp_count * piece)
        bounds = (s_rows[:1] // BK, i_rows[-1:] // BK, i_rows[:1], s_rows[-1:])
        lanes = lambda v: jnp.broadcast_to(v[:, None], (v.shape[0], HD))
        chunk_inputs.append((q_rows, lanes(s_rows), lanes(i_rows), bounds))
    chunk_inputs = lax.optimization_barrier(chunk_inputs)
    outputs = []
    for q_rows, s_rows, i_rows, bounds in chunk_inputs:
        partial_out = flash_attention(q_rows, s_rows, i_rows, gathered, w_out, bounds)
        received = lax.all_to_all(
            partial_out, ("tpz", "tpx"), split_axis=0, concat_axis=0, tiled=True
        ).reshape(tp_count, piece, -1)
        summed = received[0].astype(jnp.float32)
        for t in range(1, tp_count):
            summed = summed + received[t].astype(jnp.float32)
        outputs.append(summed.astype(jnp.bfloat16))
    attended = jnp.stack(outputs, axis=0).reshape(-1, outputs[0].shape[1])

    cache_width = 2 * HD // sharing
    cache_column = tp_rank % sharing * cache_width
    slots_here = row_count // PAGE
    page_total = page_slots.shape[0]
    wanted = seq_rank * slots_here + jnp.arange(slots_here, dtype=jnp.int32)
    page_of_slot = jnp.sum(
        jnp.where(
            page_slots[None, :] == wanted[:, None],
            jnp.arange(page_total, dtype=jnp.int32)[None, :],
            0,
        ),
        axis=1,
    )
    pages = [
        lax.dynamic_slice(gathered, (page_of_slot[j] * PAGE, cache_column), (PAGE, cache_width))
        for j in range(slots_here)
    ]
    cache_here = jnp.stack(pages, axis=0)
    return (attended, cache_here)


def solution(mesh):
    seq_size, tp_size = mesh.devices.shape
    split_mesh = jax.sharding.Mesh(
        mesh.devices.reshape(seq_size, tp_size // 2, 2), ("seq", "tpz", "tpx")
    )
    tp = ("tpz", "tpx")
    placed = (P("seq", None), P(), P(None, tp), P(), P(), P(tp, None), P(), P())
    return jax.shard_map(
        on_device,
        mesh=split_mesh,
        in_specs=placed,
        out_specs=(P(("seq",) + tp, None), P("seq", None, tp)),
        check_vma=False,
    )
```
